128 devices in a mesh: dp: 4 (over x), seq: 8 (over z, core), expert: 4 (over y).
Axes of the slice: x: 4, y: 4, z: 4, core: 2. Of those that a mesh axis runs over, the one named last changes fastest.
Arguments:
- x_in: bfloat16 [4096, 8192], P(('dp', 'seq'), 'expert'), parts along dimension 0, may hold values from -6 to 6
- z_in: bfloat16 [4096, 8192], P(('dp', 'seq'), 'expert'), parts along dimension 0, may hold values from -6 to 6
- step_raw: bfloat16 [4096, 8192], P(('dp', 'seq'), 'expert'), parts along dimension 0, may hold values from -4 to 4
- step_bias: float32 [8192], P('expert'), may hold values from -9 to -2
- decay_rate: float32 [16, 8192], P(None, 'expert'), may hold values from 0.5 to 4
- b_coef: bfloat16 [16, 4096], P(None, ('dp', 'seq')), parts along dimension 1, may hold values from -6 to 6
- c_coef: bfloat16 [16, 4096], P(None, ('dp', 'seq')), parts along dimension 1, may hold values from -6 to 6
- skip_gain: float32 [8192], P('expert'), may hold values from 0.5 to 1.5
- out_proj: bfloat16 [8192, 8192], P('expert', 'seq'), may hold values from -0.0625 to 0.0625
- residual: bfloat16 [4096, 8192], P(('dp', 'seq', 'expert')), parts along dimension 0, may hold values from -6 to 6
- norm_gain: float32 [8192], replicated, may hold values from 0.5 to 1.5
- router_weight: bfloat16 [8192, 16], replicated, may hold values from -0.0625 to 0.0625
- expert_ids: int32 [4096, 2], P(('dp', 'seq', 'expert')), parts along dimension 0, may hold values from 0 to 15, as said below
- gate_weight: bfloat16 [8192, 12288], P(None, ('seq', 'expert')), may hold values from -0.0625 to 0.0625
- up_weight: bfloat16 [8192, 12288], P(None, ('seq', 'expert')), may hold values from -0.0625 to 0.0625
- down_weight: bfloat16 [12288, 8192], P(('seq', 'expert')), may hold values from -0.0546875 to 0.0546875
Outputs:
- final: bfloat16 [4096, 8192], P(('dp', 'seq', 'expert')), parts along dimension 0
The draws below stay inside these ranges and needn't reach their ends.
There are 4 independent parts, one for each index of `dp`. The reference program is written for one: setup_inputs(seed, part) draws one part's arguments, and reference() takes and returns one part's arrays. A program takes and returns all parts, laid end to end along the dimension named above; an argument that names none is the same for every part. Nothing has to cross between parts.
Inputs may be any that keep to these rules, and one draw needn't show every extreme that they name: `expert_ids`: each token names 2 different experts; among the 32 rows of one device at most 16 name expert 0 and at least one does; on some device exactly 16 do.
All inputs are finite; a program needn't handle non-finite values.
Results may differ from the reference program's by a relative error of at most 0.006.
Values may be sent and summed in bfloat16 or wider, within the bound.
No kernel may reach another device: no remote copies, remote signals or barrier semaphores. Data moves between devices by JAX's collectives and lax.ppermute only.
A program may use at most 192 MiB of HBM per device.

```python
import math
import jax
import jax.numpy as jnp
from jax import lax

D = 8192
INNER = 8192
STATE = 16
HID = 12288
EXPERTS = 16
BLOCK = 128
SEQ_LEN = 1024
ROWS = 32
CAP = 16


def draw_expert_ids(key, part):
    block_count = SEQ_LEN // ROWS
    key_list = jax.random.split(key, 6)
    zero_counts = jax.random.randint(key_list[0], (block_count,), 1, CAP + 1)
    full_block = jax.random.randint(key_list[1], (), 0, block_count)
    zero_counts = jnp.where(jnp.arange(block_count) == full_block, CAP, zero_counts)
    row_scores = jax.random.randint(key_list[2], (block_count, ROWS), 0, 65536) * ROWS + jnp.arange(ROWS, dtype=jnp.int32)[None, :]
    row_order = jnp.argsort(row_scores, axis=1)
    row_ranks = jnp.argsort(row_order, axis=1)
    picked = (row_ranks < zero_counts[:, None]).reshape(SEQ_LEN)
    first_pick = jax.random.randint(key_list[3], (SEQ_LEN,), 1, EXPERTS)
    second_pick = jax.random.randint(key_list[4], (SEQ_LEN,), 1, EXPERTS - 1)
    second_pick = second_pick + (second_pick >= first_pick).astype(jnp.int32)
    which_side = jax.random.randint(key_list[5], (SEQ_LEN,), 0, 2)
    column_zero = jnp.where(picked, jnp.where(which_side == 0, 0, first_pick), first_pick)
    column_one = jnp.where(picked, jnp.where(which_side == 0, first_pick, 0), second_pick)
    return jnp.stack([column_zero, column_one], axis=1).astype(jnp.int32)


def levels(stream_key, shape, cuts, least, top_value):
    def one(axis_at, blocks):
        steps = jax.random.uniform(jax.random.fold_in(jax.random.fold_in(stream_key, 6), axis_at), (blocks,), jnp.float32, least / len(cuts), top_value / len(cuts))
        return jnp.repeat(jnp.exp(steps), shape[axis_at] // blocks).reshape((-1,) + (1,) * (len(shape) - axis_at - 1))

    gain = one(*cuts[0])
    for cut in cuts[1:]:
        gain = gain * one(*cut)
    return gain


def scatter_about(rng, dims, scale, most, pieces=(), kind=jnp.bfloat16):
    factor_of = levels(rng, dims, pieces, -0.22, 0.18) if pieces else 1.0
    entries = jax.random.normal(rng, dims, jnp.float32) * scale * factor_of
    return jnp.minimum(jnp.maximum(entries, -most), most).astype(kind)


def setup_inputs(seed: int = 0, part: int = 0) -> dict:
    streams_of = jax.random.split(jax.random.key(seed), 17)
    part_keys = jax.random.split(jax.random.fold_in(streams_of[16], part), 17)
    x_in = scatter_about(part_keys[0], (SEQ_LEN, INNER), 1.0, 6.0, ((0, 8), (1, 4)))
    z_in = scatter_about(part_keys[1], (SEQ_LEN, INNER), 1.0, 6.0, ((0, 8), (1, 4)))
    step_raw = scatter_about(part_keys[2], (SEQ_LEN, INNER), 1.0, 4.0, ((0, 8), (1, 4)))
    step_bias = jnp.clip(-9.0 + 7.0 * jax.random.uniform(streams_of[3], (INNER,), jnp.float32) ** levels(streams_of[3], (INNER,), ((0, 4),), -0.2, 0.2), -9.0, -2.0)
    decay_rate = jnp.clip(jnp.exp(math.log(4.0) - 2.0794415 * jax.random.uniform(streams_of[4], (STATE, INNER), jnp.float32) ** levels(streams_of[4], (STATE, INNER), ((1, 4),), -0.2, 0.2)), 0.5, 4.0)
    b_coef = scatter_about(part_keys[5], (STATE, SEQ_LEN), 1.0, 6.0, ((1, 8),))
    c_coef = scatter_about(part_keys[6], (STATE, SEQ_LEN), 1.0, 6.0, ((1, 8),))
    skip_gain = jnp.clip(0.5 + 1.0 * jax.random.uniform(streams_of[7], (INNER,), jnp.float32) ** levels(streams_of[7], (INNER,), ((0, 4),), -0.2, 0.2), 0.5, 1.5)
    out_proj = scatter_about(streams_of[8], (INNER, D), INNER ** -0.5, 0.0625, ((0, 4), (1, 8)))
    residual = scatter_about(part_keys[9], (SEQ_LEN, D), 1.0, 6.0, ((0, 32),))
    norm_gain = jnp.clip(1.0 + 0.1 * jax.random.normal(streams_of[10], (D,), jnp.float32), 0.5, 1.5)
    router_weight = scatter_about(streams_of[11], (D, EXPERTS), D ** -0.5, 0.0625)
    expert_ids = draw_expert_ids(jax.random.fold_in(jax.random.fold_in(streams_of[16], part), 71), part)
    gate_weight = scatter_about(streams_of[13], (D, HID), D ** -0.5, 0.0625, ((1, 32),))
    up_weight = scatter_about(streams_of[14], (D, HID), D ** -0.5, 0.0625, ((1, 32),))
    down_weight = scatter_about(streams_of[15], (HID, D), HID ** -0.5, 0.0546875, ((0, 32),))
    return {"x_in": x_in, "z_in": z_in, "step_raw": step_raw, "step_bias": step_bias, "decay_rate": decay_rate, "b_coef": b_coef, "c_coef": c_coef, "skip_gain": skip_gain, "out_proj": out_proj, "residual": residual, "norm_gain": norm_gain, "router_weight": router_weight, "expert_ids": expert_ids, "gate_weight": gate_weight, "up_weight": up_weight, "down_weight": down_weight}


def reference(x_in, z_in, step_raw, step_bias, decay_rate, b_coef, c_coef, skip_gain, out_proj, residual, norm_gain, router_weight, expert_ids, gate_weight, up_weight, down_weight):
    step_size = jax.nn.softplus(step_raw.astype(jnp.float32) + step_bias[None, :])
    x_float = x_in.astype(jnp.float32)

    def advance(state, inputs):
        step_now, x_now, b_now, c_now = inputs
        state = jnp.exp(-step_now[None, :] * decay_rate) * state + (step_now * x_now)[None, :] * b_now[:, None]
        y_now = lax.optimization_barrier(jnp.sum(c_now[:, None] * state, axis=0)) + skip_gain * x_now
        return (state, y_now)
    start_state = jnp.zeros((STATE, INNER), jnp.float32)
    _, scanned = lax.scan(advance, start_state, (step_size, x_float, b_coef.astype(jnp.float32).T, c_coef.astype(jnp.float32).T))
    gated = (scanned * jax.nn.silu(z_in.astype(jnp.float32))).astype(jnp.bfloat16)
    mamba_out = jnp.dot(gated, out_proj, preferred_element_type=jnp.float32)
    hidden = (residual.astype(jnp.float32) + mamba_out).astype(jnp.bfloat16)
    hidden_f = hidden.astype(jnp.float32)
    normed = hidden_f * lax.rsqrt(lax.optimization_barrier(jnp.mean(hidden_f * hidden_f, axis=-1, keepdims=True)) + 1e-05) * norm_gain[None, :]
    blocked = normed.reshape(SEQ_LEN, D // BLOCK, BLOCK)
    scales = (lax.optimization_barrier(jnp.max(jnp.abs(blocked), axis=-1)) / 448.0 + 1e-06).astype(jnp.bfloat16)
    quant = (blocked / scales.astype(jnp.float32)[..., None]).astype(jnp.bfloat16)
    restored = (quant.astype(jnp.float32) * scales.astype(jnp.float32)[..., None]).astype(jnp.bfloat16).reshape(SEQ_LEN, D)
    probs = jax.nn.sigmoid(jnp.dot(restored, router_weight, preferred_element_type=jnp.float32))
    picks = expert_ids[:, :, None] == jnp.arange(EXPERTS, dtype=jnp.int32)[None, None, :]
    chosen = lax.optimization_barrier(jnp.sum(jnp.where(picks, probs[:, None, :], jnp.float32(0.0)), axis=-1))
    weights = chosen / lax.optimization_barrier(jnp.sum(chosen, axis=-1, keepdims=True))
    coef = lax.optimization_barrier(jnp.sum(jnp.where(expert_ids == 0, weights, jnp.float32(0.0)), axis=1))
    gate_value = jnp.dot(restored, gate_weight, preferred_element_type=jnp.float32)
    up_value = jnp.dot(restored, up_weight, preferred_element_type=jnp.float32)
    active = (jax.nn.silu(gate_value) * up_value).astype(jnp.bfloat16)
    expert_out = jnp.dot(active, down_weight, preferred_element_type=jnp.float32).astype(jnp.bfloat16)
    expert_out = lax.optimization_barrier(expert_out)
    return (hidden_f + coef[:, None] * expert_out.astype(jnp.float32)).astype(jnp.bfloat16)
```

```python
import jax
import jax.numpy as jnp
from jax import lax
from jax.sharding import PartitionSpec as P

BLOCK = 128


def entering(value, axis, join, neutral):
    count, mine = (lax.axis_size(axis), lax.axis_index(axis))
    stacked = lax.all_gather(jnp.stack(value), axis)
    running = tuple(jnp.full_like(part, zero) for part, zero in zip(value, neutral))
    for position in range(count - 1):
        longer = join(running, (stacked[position, 0], stacked[position, 1]))
        running = tuple(jnp.where(position < mine, new, old) for new, old in zip(longer, running))
    return running


def pair_combine(early, later):
    return (early[0] * later[0], later[0] * early[1] + later[1])


def end_state(step_size, x_float, decay_rate, b_rows):

    def end_advance(state, inputs):
        step_now, x_now, b_now = inputs
        state = (
            jnp.exp(-step_now[None, :] * decay_rate) * state
            + (step_now * x_now)[None, :] * b_now[:, None]
        )
        return (state, None)

    start_state = jnp.zeros(decay_rate.shape, jnp.float32)
    final_state, _ = lax.scan(end_advance, start_state, (step_size, x_float, b_rows), unroll=8)
    return final_state


def scan_outputs(state_in, step_size, x_float, decay_rate, b_rows, c_rows, skip_gain):

    def scan_advance(state, inputs):
        step_now, x_now, b_now, c_now = inputs
        state = (
            jnp.exp(-step_now[None, :] * decay_rate) * state
            + (step_now * x_now)[None, :] * b_now[:, None]
        )
        y_now = jnp.sum(c_now[:, None] * state, axis=0) + skip_gain * x_now
        return (state, y_now)

    _, outputs = lax.scan(scan_advance, state_in, (step_size, x_float, b_rows, c_rows), unroll=8)
    return outputs


def on_device(
    x_in,
    z_in,
    step_raw,
    step_bias,
    decay_rate,
    b_coef,
    c_coef,
    skip_gain,
    out_proj,
    residual,
    norm_gain,
    router_weight,
    expert_ids,
    gate_weight,
    up_weight,
    down_weight,
):
    step_size = jax.nn.softplus(step_raw.astype(jnp.float32) + step_bias[None, :])
    x_float = x_in.astype(jnp.float32)
    b_rows = b_coef.astype(jnp.float32).T
    c_rows = c_coef.astype(jnp.float32).T
    state_end = end_state(step_size, x_float, decay_rate, b_rows)
    decay_end = jnp.exp(-decay_rate * jnp.sum(step_size, axis=0)[None, :])
    identity = (1.0, 0.0)
    carried = entering((decay_end, state_end), "seq", pair_combine, identity)
    state_in = carried[1]
    scanned = scan_outputs(state_in, step_size, x_float, decay_rate, b_rows, c_rows, skip_gain)
    gated = (scanned * jax.nn.silu(z_in.astype(jnp.float32))).astype(jnp.bfloat16)
    seq_count = lax.axis_size("seq")
    expert_count = lax.axis_size("expert")
    rows = residual.shape[0]
    gathered = lax.all_gather(gated, "seq", axis=0, tiled=True)
    gathered = gathered.reshape(seq_count, expert_count, rows, gated.shape[1])
    gathered = jnp.transpose(gathered, (1, 0, 2, 3)).reshape(-1, gated.shape[1])
    column_part = jnp.dot(gathered, out_proj, preferred_element_type=jnp.float32)
    summed = lax.psum_scatter(column_part, "expert", scatter_dimension=0, tiled=True)
    summed = summed.reshape(seq_count, rows, column_part.shape[1])
    swapped = lax.all_to_all(summed, "seq", split_axis=0, concat_axis=0, tiled=True)
    mamba_out = jnp.transpose(swapped, (1, 0, 2)).reshape(rows, -1)
    hidden = (residual.astype(jnp.float32) + mamba_out).astype(jnp.bfloat16)
    hidden_f = hidden.astype(jnp.float32)
    width_d = hidden.shape[1]
    scale_cols = width_d // BLOCK
    normed = (
        hidden_f
        * lax.rsqrt(jnp.mean(hidden_f * hidden_f, axis=-1, keepdims=True) + 1e-05)
        * norm_gain[None, :]
    )
    blocked = normed.reshape(rows, scale_cols, BLOCK)
    scales = (jnp.max(jnp.abs(blocked), axis=-1) / 448.0 + 1e-06).astype(jnp.bfloat16)
    quant = (blocked / scales.astype(jnp.float32)[..., None]).astype(jnp.bfloat16)
    restored = (
        (quant.astype(jnp.float32) * scales.astype(jnp.float32)[..., None])
        .astype(jnp.bfloat16)
        .reshape(rows, width_d)
    )
    experts = router_weight.shape[1]
    probs = jax.nn.sigmoid(jnp.dot(restored, router_weight, preferred_element_type=jnp.float32))
    picks = expert_ids[:, :, None] == jnp.arange(experts, dtype=jnp.int32)[None, None, :]
    chosen = jnp.sum(jnp.where(picks, probs[:, None, :], jnp.float32(0.0)), axis=-1)
    weights = chosen / jnp.sum(chosen, axis=-1, keepdims=True)
    coef = jnp.sum(jnp.where(expert_ids == 0, weights, jnp.float32(0.0)), axis=1)
    wanted = jnp.any(expert_ids == 0, axis=1)
    wanted_int = wanted.astype(jnp.int32)
    slot_pos = jnp.cumsum(wanted_int) - wanted_int
    capacity = rows // 2
    table = (
        (slot_pos[None, :] == jnp.arange(capacity, dtype=jnp.int32)[:, None]) & wanted[None, :]
    ).astype(jnp.bfloat16)
    send_rows = jnp.dot(table, restored, preferred_element_type=jnp.float32).astype(jnp.bfloat16)
    inputs = lax.all_gather(send_rows, ("seq", "expert"), axis=0, tiled=True)
    gate_value = jnp.dot(inputs, gate_weight, preferred_element_type=jnp.float32)
    up_value = jnp.dot(inputs, up_weight, preferred_element_type=jnp.float32)
    active = (jax.nn.silu(gate_value) * up_value).astype(jnp.bfloat16)
    own_sum = lax.psum_scatter(
        jnp.dot(active, down_weight, preferred_element_type=jnp.float32).astype(jnp.bfloat16),
        ("seq", "expert"),
        scatter_dimension=0,
        tiled=True,
    )
    returned = jnp.dot(table.T, own_sum, preferred_element_type=jnp.float32)
    return (hidden_f + coef[:, None] * returned).astype(jnp.bfloat16)


def solution(mesh):
    return jax.shard_map(
        on_device,
        mesh=mesh,
        in_specs=(
            P(("dp", "seq"), "expert"),
            P(("dp", "seq"), "expert"),
            P(("dp", "seq"), "expert"),
            P("expert"),
            P(None, "expert"),
            P(None, ("dp", "seq")),
            P(None, ("dp", "seq")),
            P("expert"),
            P("expert", "seq"),
            P(("dp", "seq", "expert"), None),
            P(),
            P(),
            P(("dp", "seq", "expert"), None),
            P(None, ("seq", "expert")),
            P(None, ("seq", "expert")),
            P(("seq", "expert"), None),
        ),
        out_specs=P(("dp", "seq", "expert"), None),
        check_vma=False,
    )
```

```python
import jax
import jax.numpy as jnp
from jax import lax
from jax.experimental import pallas as pl
from jax.experimental.pallas import tpu as pltpu
from jax.sharding import PartitionSpec as P

BLOCK = 128
LANES = 128
ROWS_PER_LOAD = 16


def _lane_tile(col, width):
    return jnp.concatenate([col] * (width // LANES), axis=1) if width > LANES else col


def _end_kernel(step_ref, x_ref, decay_ref, b_ref, state_ref):
    steps, width = step_ref.shape
    rate = decay_ref[...]

    def body(k, state):
        base = pl.multiple_of(k * ROWS_PER_LOAD, ROWS_PER_LOAD)
        s_blk = step_ref[pl.ds(base, ROWS_PER_LOAD), :]
        x_blk = x_ref[pl.ds(base, ROWS_PER_LOAD), :].astype(jnp.float32)
        for i in range(ROWS_PER_LOAD):
            s_now = s_blk[i : i + 1]
            b_now = _lane_tile(b_ref[base + i], width)
            state = jnp.exp(-s_now * rate) * state + (s_now * x_blk[i : i + 1]) * b_now
        return state

    zero = jnp.zeros(rate.shape, jnp.float32)
    state_ref[...] = lax.fori_loop(0, steps // ROWS_PER_LOAD, body, zero)


def _out_kernel(state_in_ref, step_ref, x_ref, z_ref, decay_ref, b_ref, c_ref, skip_ref, gated_ref, y_ref):
    steps, width = step_ref.shape
    rate = decay_ref[...]
    skip = skip_ref[...]

    def body(k, state):
        base = pl.multiple_of(k * ROWS_PER_LOAD, ROWS_PER_LOAD)
        s_blk = step_ref[pl.ds(base, ROWS_PER_LOAD), :]
        x_blk = x_ref[pl.ds(base, ROWS_PER_LOAD), :].astype(jnp.float32)
        for i in range(ROWS_PER_LOAD):
            s_now = s_blk[i : i + 1]
            x_now = x_blk[i : i + 1]
            b_now = _lane_tile(b_ref[base + i], width)
            c_now = _lane_tile(c_ref[base + i], width)
            state = jnp.exp(-s_now * rate) * state + (s_now * x_now) * b_now
            y_ref[pl.ds(base + i, 1), :] = jnp.sum(c_now * state, axis=0, keepdims=True) + skip * x_now
        return state

    lax.fori_loop(0, steps // ROWS_PER_LOAD, body, state_in_ref[...])
    z = z_ref[...].astype(jnp.float32)
    gated_ref[...] = (y_ref[...] * (z * jax.nn.sigmoid(z))).astype(gated_ref.dtype)


def _columns(b_coef):
    rows = b_coef.astype(jnp.float32).T
    return jnp.broadcast_to(rows[:, :, None], rows.shape + (LANES,))


def scan_end(step_size, x_in, decay_rate, b_coef, width=512):
    steps, chans = step_size.shape
    states = decay_rate.shape[0]
    grid = (chans // width,)
    return pl.pallas_call(
        _end_kernel,
        grid=grid,
        in_specs=[
            pl.BlockSpec((steps, width), lambda j: (0, j)),
            pl.BlockSpec((steps, width), lambda j: (0, j)),
            pl.BlockSpec((states, width), lambda j: (0, j)),
            pl.BlockSpec((steps, states, LANES), lambda j: (0, 0, 0)),
        ],
        out_specs=pl.BlockSpec((states, width), lambda j: (0, j)),
        out_shape=jax.ShapeDtypeStruct((states, chans), jnp.float32),
        cost_estimate=pl.CostEstimate(
            flops=6 * steps * states * chans, transcendentals=steps * states * chans,
            bytes_accessed=steps * chans * 6 + states * chans * 8),
    )(step_size, x_in, decay_rate, _columns(b_coef))


def scan_gated(state_in, step_size, x_in, z_in, decay_rate, b_coef, c_coef, skip_gain, width=512):
    steps, chans = step_size.shape
    states = decay_rate.shape[0]
    grid = (chans // width,)
    col = lambda j: (0, j)
    return pl.pallas_call(
        _out_kernel,
        grid=grid,
        in_specs=[
            pl.BlockSpec((states, width), col),
            pl.BlockSpec((steps, width), col),
            pl.BlockSpec((steps, width), col),
            pl.BlockSpec((steps, width), col),
            pl.BlockSpec((states, width), col),
            pl.BlockSpec((steps, states, LANES), lambda j: (0, 0, 0)),
            pl.BlockSpec((steps, states, LANES), lambda j: (0, 0, 0)),
            pl.BlockSpec((1, width), col),
        ],
        out_specs=pl.BlockSpec((steps, width), col),
        out_shape=jax.ShapeDtypeStruct((steps, chans), jnp.bfloat16),
        scratch_shapes=[pltpu.VMEM((steps, width), jnp.float32)],
        cost_estimate=pl.CostEstimate(
            flops=9 * steps * states * chans, transcendentals=steps * states * chans + steps * chans,
            bytes_accessed=steps * chans * 10 + states * chans * 8),
    )(state_in, step_size, x_in, z_in, decay_rate, _columns(b_coef), _columns(c_coef), skip_gain[None, :])


def entering(value, axis, join, neutral):
    count, mine = (lax.axis_size(axis), lax.axis_index(axis))
    stacked = lax.all_gather(jnp.stack(value), axis)
    running = tuple(jnp.full_like(part, zero) for part, zero in zip(value, neutral))
    for position in range(count - 1):
        longer = join(running, (stacked[position, 0], stacked[position, 1]))
        running = tuple(jnp.where(position < mine, new, old) for new, old in zip(longer, running))
    return running


def pair_combine(early, later):
    return (early[0] * later[0], later[0] * early[1] + later[1])


def end_state(step_size, x_float, decay_rate, b_rows):

    def end_advance(state, inputs):
        step_now, x_now, b_now = inputs
        state = (
            jnp.exp(-step_now[None, :] * decay_rate) * state
            + (step_now * x_now)[None, :] * b_now[:, None]
        )
        return (state, None)

    start_state = jnp.zeros(decay_rate.shape, jnp.float32)
    final_state, _ = lax.scan(end_advance, start_state, (step_size, x_float, b_rows), unroll=8)
    return final_state


def scan_outputs(state_in, step_size, x_float, decay_rate, b_rows, c_rows, skip_gain):

    def scan_advance(state, inputs):
        step_now, x_now, b_now, c_now = inputs
        state = (
            jnp.exp(-step_now[None, :] * decay_rate) * state
            + (step_now * x_now)[None, :] * b_now[:, None]
        )
        y_now = jnp.sum(c_now[:, None] * state, axis=0) + skip_gain * x_now
        return (state, y_now)

    _, outputs = lax.scan(scan_advance, state_in, (step_size, x_float, b_rows, c_rows), unroll=8)
    return outputs


def on_device(
    x_in,
    z_in,
    step_raw,
    step_bias,
    decay_rate,
    b_coef,
    c_coef,
    skip_gain,
    out_proj,
    residual,
    norm_gain,
    router_weight,
    expert_ids,
    gate_weight,
    up_weight,
    down_weight,
):
    step_size = jax.nn.softplus(step_raw.astype(jnp.float32) + step_bias[None, :])
    x_float = x_in.astype(jnp.float32)
    state_end = scan_end(step_size, x_in, decay_rate, b_coef)
    decay_end = jnp.exp(-decay_rate * jnp.sum(step_size, axis=0)[None, :])
    identity = (1.0, 0.0)
    carried = entering((decay_end, state_end), "seq", pair_combine, identity)
    state_in = carried[1]
    gated = scan_gated(state_in, step_size, x_in, z_in, decay_rate, b_coef, c_coef, skip_gain)
    seq_count = lax.axis_size("seq")
    expert_count = lax.axis_size("expert")
    rows = residual.shape[0]
    gathered = lax.all_gather(gated, "seq", axis=0, tiled=True)
    gathered = gathered.reshape(seq_count, expert_count, rows, gated.shape[1])
    gathered = jnp.transpose(gathered, (1, 0, 2, 3)).reshape(-1, gated.shape[1])
    column_part = jnp.dot(gathered, out_proj, preferred_element_type=jnp.float32)
    summed = lax.psum_scatter(column_part, "expert", scatter_dimension=0, tiled=True)
    summed = summed.reshape(seq_count, rows, column_part.shape[1])
    swapped = lax.all_to_all(summed, "seq", split_axis=0, concat_axis=0, tiled=True)
    mamba_out = jnp.transpose(swapped, (1, 0, 2)).reshape(rows, -1)
    hidden = (residual.astype(jnp.float32) + mamba_out).astype(jnp.bfloat16)
    hidden_f = hidden.astype(jnp.float32)
    width_d = hidden.shape[1]
    scale_cols = width_d // BLOCK
    normed = (
        hidden_f
        * lax.rsqrt(jnp.mean(hidden_f * hidden_f, axis=-1, keepdims=True) + 1e-05)
        * norm_gain[None, :]
    )
    blocked = normed.reshape(rows, scale_cols, BLOCK)
    scales = (jnp.max(jnp.abs(blocked), axis=-1) / 448.0 + 1e-06).astype(jnp.bfloat16)
    quant = (blocked / scales.astype(jnp.float32)[..., None]).astype(jnp.bfloat16)
    restored = (
        (quant.astype(jnp.float32) * scales.astype(jnp.float32)[..., None])
        .astype(jnp.bfloat16)
        .reshape(rows, width_d)
    )
    experts = router_weight.shape[1]
    probs = jax.nn.sigmoid(jnp.dot(restored, router_weight, preferred_element_type=jnp.float32))
    picks = expert_ids[:, :, None] == jnp.arange(experts, dtype=jnp.int32)[None, None, :]
    chosen = jnp.sum(jnp.where(picks, probs[:, None, :], jnp.float32(0.0)), axis=-1)
    weights = chosen / jnp.sum(chosen, axis=-1, keepdims=True)
    coef = jnp.sum(jnp.where(expert_ids == 0, weights, jnp.float32(0.0)), axis=1)
    wanted = jnp.any(expert_ids == 0, axis=1)
    wanted_int = wanted.astype(jnp.int32)
    slot_pos = jnp.cumsum(wanted_int) - wanted_int
    capacity = rows // 2
    table = (
        (slot_pos[None, :] == jnp.arange(capacity, dtype=jnp.int32)[:, None]) & wanted[None, :]
    ).astype(jnp.bfloat16)
    send_rows = jnp.dot(table, restored, preferred_element_type=jnp.float32).astype(jnp.bfloat16)
    inputs = lax.all_gather(send_rows, ("seq", "expert"), axis=0, tiled=True)
    gate_value = jnp.dot(inputs, gate_weight, preferred_element_type=jnp.float32)
    up_value = jnp.dot(inputs, up_weight, preferred_element_type=jnp.float32)
    active = (jax.nn.silu(gate_value) * up_value).astype(jnp.bfloat16)
    own_sum = lax.psum_scatter(
        jnp.dot(active, down_weight, preferred_element_type=jnp.float32).astype(jnp.bfloat16),
        ("seq", "expert"),
        scatter_dimension=0,
        tiled=True,
    )
    returned = jnp.dot(table.T, own_sum, preferred_element_type=jnp.float32)
    return (hidden_f + coef[:, None] * returned).astype(jnp.bfloat16)


def solution(mesh):
    return jax.shard_map(
        on_device,
        mesh=mesh,
        in_specs=(
            P(("dp", "seq"), "expert"),
            P(("dp", "seq"), "expert"),
            P(("dp", "seq"), "expert"),
            P("expert"),
            P(None, "expert"),
            P(None, ("dp", "seq")),
            P(None, ("dp", "seq")),
            P("expert"),
            P("expert", "seq"),
            P(("dp", "seq", "expert"), None),
            P(),
            P(),
            P(("dp", "seq", "expert"), None),
            P(None, ("seq", "expert")),
            P(None, ("seq", "expert")),
            P(("seq", "expert"), None),
        ),
        out_specs=P(("dp", "seq", "expert"), None),
        check_vma=False,
    )
```

```python
import jax
import jax.numpy as jnp
from jax import lax
from jax.experimental import pallas as pl
from jax.experimental.pallas import tpu as pltpu
from jax.sharding import PartitionSpec as P

BLOCK = 128
LANES = 128
ROWS_PER_LOAD = 16


def _lane_tile(col, width):
    return jnp.concatenate([col] * (width // LANES), axis=1) if width > LANES else col


def _end_kernel(step_ref, x_ref, decay_ref, b_ref, state_ref):
    steps, width = step_ref.shape
    rate = decay_ref[...]

    def body(k, state):
        base = pl.multiple_of(k * ROWS_PER_LOAD, ROWS_PER_LOAD)
        s_blk = step_ref[pl.ds(base, ROWS_PER_LOAD), :]
        x_blk = x_ref[pl.ds(base, ROWS_PER_LOAD), :].astype(jnp.float32)
        for i in range(ROWS_PER_LOAD):
            s_now = s_blk[i : i + 1]
            b_now = _lane_tile(b_ref[base + i], width)
            state = jnp.exp(-s_now * rate) * state + (s_now * x_blk[i : i + 1]) * b_now
        return state

    zero = jnp.zeros(rate.shape, jnp.float32)
    state_ref[...] = lax.fori_loop(0, steps // ROWS_PER_LOAD, body, zero)


def _out_kernel(state_in_ref, step_ref, x_ref, z_ref, decay_ref, b_ref, c_ref, skip_ref, gated_ref, y_ref):
    steps, width = step_ref.shape
    rate = decay_ref[...]
    skip = skip_ref[...]

    def body(k, state):
        base = pl.multiple_of(k * ROWS_PER_LOAD, ROWS_PER_LOAD)
        s_blk = step_ref[pl.ds(base, ROWS_PER_LOAD), :]
        x_blk = x_ref[pl.ds(base, ROWS_PER_LOAD), :].astype(jnp.float32)
        for i in range(ROWS_PER_LOAD):
            s_now = s_blk[i : i + 1]
            x_now = x_blk[i : i + 1]
            b_now = _lane_tile(b_ref[base + i], width)
            c_now = _lane_tile(c_ref[base + i], width)
            state = jnp.exp(-s_now * rate) * state + (s_now * x_now) * b_now
            y_ref[pl.ds(base + i, 1), :] = jnp.sum(c_now * state, axis=0, keepdims=True) + skip * x_now
        return state

    lax.fori_loop(0, steps // ROWS_PER_LOAD, body, state_in_ref[...])
    z = z_ref[...].astype(jnp.float32)
    gated_ref[...] = (y_ref[...] * (z * jax.nn.sigmoid(z))).astype(gated_ref.dtype)


def _columns(b_coef):
    rows = b_coef.astype(jnp.float32).T
    return jnp.broadcast_to(rows[:, :, None], rows.shape + (LANES,))


def scan_end(step_size, x_in, decay_rate, b_coef, width=512):
    steps, chans = step_size.shape
    states = decay_rate.shape[0]
    grid = (chans // width,)
    return pl.pallas_call(
        _end_kernel,
        grid=grid,
        in_specs=[
            pl.BlockSpec((steps, width), lambda j: (0, j)),
            pl.BlockSpec((steps, width), lambda j: (0, j)),
            pl.BlockSpec((states, width), lambda j: (0, j)),
            pl.BlockSpec((steps, states, LANES), lambda j: (0, 0, 0)),
        ],
        out_specs=pl.BlockSpec((states, width), lambda j: (0, j)),
        out_shape=jax.ShapeDtypeStruct((states, chans), jnp.float32),
        cost_estimate=pl.CostEstimate(
            flops=6 * steps * states * chans, transcendentals=steps * states * chans,
            bytes_accessed=steps * chans * 6 + states * chans * 8),
    )(step_size, x_in, decay_rate, _columns(b_coef))


def scan_gated(state_in, step_size, x_in, z_in, decay_rate, b_coef, c_coef, skip_gain, width=512):
    steps, chans = step_size.shape
    states = decay_rate.shape[0]
    grid = (chans // width,)
    col = lambda j: (0, j)
    return pl.pallas_call(
        _out_kernel,
        grid=grid,
        in_specs=[
            pl.BlockSpec((states, width), col),
            pl.BlockSpec((steps, width), col),
            pl.BlockSpec((steps, width), col),
            pl.BlockSpec((steps, width), col),
            pl.BlockSpec((states, width), col),
            pl.BlockSpec((steps, states, LANES), lambda j: (0, 0, 0)),
            pl.BlockSpec((steps, states, LANES), lambda j: (0, 0, 0)),
            pl.BlockSpec((1, width), col),
        ],
        out_specs=pl.BlockSpec((steps, width), col),
        out_shape=jax.ShapeDtypeStruct((steps, chans), jnp.bfloat16),
        scratch_shapes=[pltpu.VMEM((steps, width), jnp.float32)],
        cost_estimate=pl.CostEstimate(
            flops=9 * steps * states * chans, transcendentals=steps * states * chans + steps * chans,
            bytes_accessed=steps * chans * 10 + states * chans * 8),
    )(state_in, step_size, x_in, z_in, decay_rate, _columns(b_coef), _columns(c_coef), skip_gain[None, :])


def entering_state(state_end, step_total, decay_rate, axis):
    count, mine = (lax.axis_size(axis), lax.axis_index(axis))
    stacked = lax.all_gather(jnp.concatenate([state_end, step_total[None, :]], axis=0), axis)
    running = jnp.zeros_like(state_end)
    for position in range(count - 1):
        decay_then = jnp.exp(-decay_rate * stacked[position, -1][None, :])
        longer = decay_then * running + stacked[position, :-1]
        running = jnp.where(position < mine, longer, running)
    return running


def on_device(
    x_in,
    z_in,
    step_raw,
    step_bias,
    decay_rate,
    b_coef,
    c_coef,
    skip_gain,
    out_proj,
    residual,
    norm_gain,
    router_weight,
    expert_ids,
    gate_weight,
    up_weight,
    down_weight,
):
    step_size = jax.nn.softplus(step_raw.astype(jnp.float32) + step_bias[None, :])
    state_end = scan_end(step_size, x_in, decay_rate, b_coef)
    state_in = entering_state(state_end, jnp.sum(step_size, axis=0), decay_rate, "seq")
    gated = scan_gated(state_in, step_size, x_in, z_in, decay_rate, b_coef, c_coef, skip_gain)
    seq_count = lax.axis_size("seq")
    expert_count = lax.axis_size("expert")
    rows = residual.shape[0]
    gathered = lax.all_gather(gated, "seq", axis=0, tiled=True)
    gathered = gathered.reshape(seq_count, expert_count, rows, gated.shape[1])
    gathered = jnp.transpose(gathered, (1, 0, 2, 3)).reshape(-1, gated.shape[1])
    column_part = jnp.dot(gathered, out_proj, preferred_element_type=jnp.float32).astype(jnp.bfloat16)
    summed = lax.psum_scatter(column_part, "expert", scatter_dimension=0, tiled=True)
    summed = summed.reshape(seq_count, rows, column_part.shape[1])
    swapped = lax.all_to_all(summed, "seq", split_axis=0, concat_axis=0, tiled=True)
    mamba_out = jnp.transpose(swapped, (1, 0, 2)).reshape(rows, -1)
    hidden = (residual.astype(jnp.float32) + mamba_out).astype(jnp.bfloat16)
    hidden_f = hidden.astype(jnp.float32)
    width_d = hidden.shape[1]
    scale_cols = width_d // BLOCK
    normed = (
        hidden_f
        * lax.rsqrt(jnp.mean(hidden_f * hidden_f, axis=-1, keepdims=True) + 1e-05)
        * norm_gain[None, :]
    )
    blocked = normed.reshape(rows, scale_cols, BLOCK)
    scales = (jnp.max(jnp.abs(blocked), axis=-1) / 448.0 + 1e-06).astype(jnp.bfloat16)
    quant = (blocked / scales.astype(jnp.float32)[..., None]).astype(jnp.bfloat16)
    restored = (
        (quant.astype(jnp.float32) * scales.astype(jnp.float32)[..., None])
        .astype(jnp.bfloat16)
        .reshape(rows, width_d)
    )
    experts = router_weight.shape[1]
    probs = jax.nn.sigmoid(jnp.dot(restored, router_weight, preferred_element_type=jnp.float32))
    picks = expert_ids[:, :, None] == jnp.arange(experts, dtype=jnp.int32)[None, None, :]
    chosen = jnp.sum(jnp.where(picks, probs[:, None, :], jnp.float32(0.0)), axis=-1)
    weights = chosen / jnp.sum(chosen, axis=-1, keepdims=True)
    coef = jnp.sum(jnp.where(expert_ids == 0, weights, jnp.float32(0.0)), axis=1)
    wanted = jnp.any(expert_ids == 0, axis=1)
    wanted_int = wanted.astype(jnp.int32)
    slot_pos = jnp.cumsum(wanted_int) - wanted_int
    capacity = rows // 2
    table = (
        (slot_pos[None, :] == jnp.arange(capacity, dtype=jnp.int32)[:, None]) & wanted[None, :]
    ).astype(jnp.bfloat16)
    send_rows = jnp.dot(table, restored, preferred_element_type=jnp.float32).astype(jnp.bfloat16)
    inputs = lax.all_gather(send_rows, ("seq", "expert"), axis=0, tiled=True)
    gate_value = jnp.dot(inputs, gate_weight, preferred_element_type=jnp.float32)
    up_value = jnp.dot(inputs, up_weight, preferred_element_type=jnp.float32)
    active = (jax.nn.silu(gate_value) * up_value).astype(jnp.bfloat16)
    own_sum = lax.psum_scatter(
        jnp.dot(active, down_weight, preferred_element_type=jnp.float32).astype(jnp.bfloat16),
        ("seq", "expert"),
        scatter_dimension=0,
        tiled=True,
    )
    returned = jnp.dot(table.T, own_sum, preferred_element_type=jnp.float32)
    return (hidden_f + coef[:, None] * returned).astype(jnp.bfloat16)


def solution(mesh):
    return jax.shard_map(
        on_device,
        mesh=mesh,
        in_specs=(
            P(("dp", "seq"), "expert"),
            P(("dp", "seq"), "expert"),
            P(("dp", "seq"), "expert"),
            P("expert"),
            P(None, "expert"),
            P(None, ("dp", "seq")),
            P(None, ("dp", "seq")),
            P("expert"),
            P("expert", "seq"),
            P(("dp", "seq", "expert"), None),
            P(),
            P(),
            P(("dp", "seq", "expert"), None),
            P(None, ("seq", "expert")),
            P(None, ("seq", "expert")),
            P(("seq", "expert"), None),
        ),
        out_specs=P(("dp", "seq", "expert"), None),
        check_vma=False,
    )
```

```python
import jax
import jax.numpy as jnp
from jax import lax
from jax.experimental import pallas as pl
from jax.experimental.pallas import tpu as pltpu
from jax.sharding import PartitionSpec as P

BLOCK = 128
LANES = 128
ROWS_PER_LOAD = 16


def _lane_tile(col, width):
    return jnp.concatenate([col] * (width // LANES), axis=1) if width > LANES else col


def _end_kernel(step_ref, x_ref, decay_ref, b_ref, state_ref):
    steps, width = step_ref.shape
    rate = decay_ref[...]

    def body(k, state):
        base = pl.multiple_of(k * ROWS_PER_LOAD, ROWS_PER_LOAD)
        s_blk = step_ref[pl.ds(base, ROWS_PER_LOAD), :]
        x_blk = x_ref[pl.ds(base, ROWS_PER_LOAD), :].astype(jnp.float32)
        for i in range(ROWS_PER_LOAD):
            s_now = s_blk[i : i + 1]
            b_now = _lane_tile(b_ref[base + i], width)
            state = jnp.exp(-s_now * rate) * state + (s_now * x_blk[i : i + 1]) * b_now
        return state

    zero = jnp.zeros(rate.shape, jnp.float32)
    state_ref[...] = lax.fori_loop(0, steps // ROWS_PER_LOAD, body, zero)


def _out_kernel(state_in_ref, step_ref, x_ref, z_ref, decay_ref, b_ref, c_ref, skip_ref, gated_ref, y_ref):
    steps, width = step_ref.shape
    rate = decay_ref[...]
    skip = skip_ref[...]

    def body(k, state):
        base = pl.multiple_of(k * ROWS_PER_LOAD, ROWS_PER_LOAD)
        s_blk = step_ref[pl.ds(base, ROWS_PER_LOAD), :]
        x_blk = x_ref[pl.ds(base, ROWS_PER_LOAD), :].astype(jnp.float32)
        for i in range(ROWS_PER_LOAD):
            s_now = s_blk[i : i + 1]
            x_now = x_blk[i : i + 1]
            b_now = _lane_tile(b_ref[base + i], width)
            c_now = _lane_tile(c_ref[base + i], width)
            state = jnp.exp(-s_now * rate) * state + (s_now * x_now) * b_now
            y_ref[pl.ds(base + i, 1), :] = jnp.sum(c_now * state, axis=0, keepdims=True) + skip * x_now
        return state

    lax.fori_loop(0, steps // ROWS_PER_LOAD, body, state_in_ref[...])
    z = z_ref[...].astype(jnp.float32)
    gated_ref[...] = (y_ref[...] * (z * jax.nn.sigmoid(z))).astype(gated_ref.dtype)


def _columns(b_coef):
    rows = b_coef.astype(jnp.float32).T
    return jnp.broadcast_to(rows[:, :, None], rows.shape + (LANES,))


def scan_end(step_size, x_in, decay_rate, b_coef, width=512):
    steps, chans = step_size.shape
    states = decay_rate.shape[0]
    grid = (chans // width,)
    return pl.pallas_call(
        _end_kernel,
        grid=grid,
        in_specs=[
            pl.BlockSpec((steps, width), lambda j: (0, j)),
            pl.BlockSpec((steps, width), lambda j: (0, j)),
            pl.BlockSpec((states, width), lambda j: (0, j)),
            pl.BlockSpec((steps, states, LANES), lambda j: (0, 0, 0)),
        ],
        out_specs=pl.BlockSpec((states, width), lambda j: (0, j)),
        out_shape=jax.ShapeDtypeStruct((states, chans), jnp.float32),
        cost_estimate=pl.CostEstimate(
            flops=6 * steps * states * chans, transcendentals=steps * states * chans,
            bytes_accessed=steps * chans * 6 + states * chans * 8),
    )(step_size, x_in, decay_rate, _columns(b_coef))


def scan_gated(state_in, step_size, x_in, z_in, decay_rate, b_coef, c_coef, skip_gain, width=512):
    steps, chans = step_size.shape
    states = decay_rate.shape[0]
    grid = (chans // width,)
    col = lambda j: (0, j)
    return pl.pallas_call(
        _out_kernel,
        grid=grid,
        in_specs=[
            pl.BlockSpec((states, width), col),
            pl.BlockSpec((steps, width), col),
            pl.BlockSpec((steps, width), col),
            pl.BlockSpec((steps, width), col),
            pl.BlockSpec((states, width), col),
            pl.BlockSpec((steps, states, LANES), lambda j: (0, 0, 0)),
            pl.BlockSpec((steps, states, LANES), lambda j: (0, 0, 0)),
            pl.BlockSpec((1, width), col),
        ],
        out_specs=pl.BlockSpec((steps, width), col),
        out_shape=jax.ShapeDtypeStruct((steps, chans), jnp.bfloat16),
        scratch_shapes=[pltpu.VMEM((steps, width), jnp.float32)],
        cost_estimate=pl.CostEstimate(
            flops=9 * steps * states * chans, transcendentals=steps * states * chans + steps * chans,
            bytes_accessed=steps * chans * 10 + states * chans * 8),
    )(state_in, step_size, x_in, z_in, decay_rate, _columns(b_coef), _columns(c_coef), skip_gain[None, :])


def entering_state(state_end, step_total, decay_rate, axis):
    count, mine = (lax.axis_size(axis), lax.axis_index(axis))
    stacked = lax.all_gather(jnp.concatenate([state_end, step_total[None, :]], axis=0), axis)
    running = jnp.zeros_like(state_end)
    for position in range(count - 1):
        decay_then = jnp.exp(-decay_rate * stacked[position, -1][None, :])
        longer = decay_then * running + stacked[position, :-1]
        running = jnp.where(position < mine, longer, running)
    return running


def on_device(
    x_in,
    z_in,
    step_raw,
    step_bias,
    decay_rate,
    b_coef,
    c_coef,
    skip_gain,
    out_proj,
    residual,
    norm_gain,
    router_weight,
    expert_ids,
    gate_weight,
    up_weight,
    down_weight,
):
    step_size = jax.nn.softplus(step_raw.astype(jnp.float32) + step_bias[None, :])
    state_end = scan_end(step_size, x_in, decay_rate, b_coef)
    state_in = entering_state(state_end, jnp.sum(step_size, axis=0), decay_rate, "seq")
    gated = scan_gated(state_in, step_size, x_in, z_in, decay_rate, b_coef, c_coef, skip_gain)
    seq_count = lax.axis_size("seq")
    expert_count = lax.axis_size("expert")
    rows = residual.shape[0]
    gathered = lax.all_gather(gated, "seq", axis=0, tiled=True)
    column_part = jnp.dot(gathered, out_proj, preferred_element_type=jnp.float32).astype(jnp.bfloat16)
    column_part = column_part.reshape(seq_count * expert_count, rows, column_part.shape[1])
    swapped = lax.all_to_all(column_part, ("seq", "expert"), split_axis=0, concat_axis=0, tiled=True)
    swapped = swapped.reshape(seq_count, expert_count, rows, column_part.shape[2])
    summed = jnp.sum(swapped.astype(jnp.float32), axis=1)
    mamba_out = jnp.transpose(summed, (1, 0, 2)).reshape(rows, -1)
    hidden = (residual.astype(jnp.float32) + mamba_out).astype(jnp.bfloat16)
    hidden_f = hidden.astype(jnp.float32)
    width_d = hidden.shape[1]
    scale_cols = width_d // BLOCK
    normed = (
        hidden_f
        * lax.rsqrt(jnp.mean(hidden_f * hidden_f, axis=-1, keepdims=True) + 1e-05)
        * norm_gain[None, :]
    )
    blocked = normed.reshape(rows, scale_cols, BLOCK)
    scales = (jnp.max(jnp.abs(blocked), axis=-1) / 448.0 + 1e-06).astype(jnp.bfloat16)
    quant = (blocked / scales.astype(jnp.float32)[..., None]).astype(jnp.bfloat16)
    restored = (
        (quant.astype(jnp.float32) * scales.astype(jnp.float32)[..., None])
        .astype(jnp.bfloat16)
        .reshape(rows, width_d)
    )
    experts = router_weight.shape[1]
    probs = jax.nn.sigmoid(jnp.dot(restored, router_weight, preferred_element_type=jnp.float32))
    picks = expert_ids[:, :, None] == jnp.arange(experts, dtype=jnp.int32)[None, None, :]
    chosen = jnp.sum(jnp.where(picks, probs[:, None, :], jnp.float32(0.0)), axis=-1)
    weights = chosen / jnp.sum(chosen, axis=-1, keepdims=True)
    coef = jnp.sum(jnp.where(expert_ids == 0, weights, jnp.float32(0.0)), axis=1)
    wanted = jnp.any(expert_ids == 0, axis=1)
    wanted_int = wanted.astype(jnp.int32)
    slot_pos = jnp.cumsum(wanted_int) - wanted_int
    capacity = rows // 2
    table = (
        (slot_pos[None, :] == jnp.arange(capacity, dtype=jnp.int32)[:, None]) & wanted[None, :]
    ).astype(jnp.bfloat16)
    send_rows = jnp.dot(table, restored, preferred_element_type=jnp.float32).astype(jnp.bfloat16)
    inputs = lax.all_gather(send_rows, ("seq", "expert"), axis=0, tiled=True)
    gate_value = jnp.dot(inputs, gate_weight, preferred_element_type=jnp.float32)
    up_value = jnp.dot(inputs, up_weight, preferred_element_type=jnp.float32)
    active = (jax.nn.silu(gate_value) * up_value).astype(jnp.bfloat16)
    own_sum = lax.psum_scatter(
        jnp.dot(active, down_weight, preferred_element_type=jnp.float32).astype(jnp.bfloat16),
        ("seq", "expert"),
        scatter_dimension=0,
        tiled=True,
    )
    returned = jnp.dot(table.T, own_sum, preferred_element_type=jnp.float32)
    return (hidden_f + coef[:, None] * returned).astype(jnp.bfloat16)


def solution(mesh):
    return jax.shard_map(
        on_device,
        mesh=mesh,
        in_specs=(
            P(("dp", "seq"), "expert"),
            P(("dp", "seq"), "expert"),
            P(("dp", "seq"), "expert"),
            P("expert"),
            P(None, "expert"),
            P(None, ("dp", "seq")),
            P(None, ("dp", "seq")),
            P("expert"),
            P("expert", "seq"),
            P(("dp", "seq", "expert"), None),
            P(),
            P(),
            P(("dp", "seq", "expert"), None),
            P(None, ("seq", "expert")),
            P(None, ("seq", "expert")),
            P(("seq", "expert"), None),
        ),
        out_specs=P(("dp", "seq", "expert"), None),
        check_vma=False,
    )
```

```python
import jax
import jax.numpy as jnp
from jax import lax
from jax.experimental import pallas as pl
from jax.experimental.pallas import tpu as pltpu
from jax.sharding import PartitionSpec as P

BLOCK = 128
LANES = 128
ROWS_PER_LOAD = 16

EXPERT_TILE = 2048


def _expert_kernel(nk, rows_ref, gate_ref, up_ref, down_ref, out_ref, acc_g, acc_u, active):
    i = pl.program_id(0)

    @pl.when(i == 0)
    def _():
        acc_g[...] = jnp.zeros_like(acc_g)
        acc_u[...] = jnp.zeros_like(acc_u)

    @pl.when(i < nk)
    def _():
        x = rows_ref[...]
        acc_g[...] += jnp.dot(x, gate_ref[...], preferred_element_type=jnp.float32)
        acc_u[...] += jnp.dot(x, up_ref[...], preferred_element_type=jnp.float32)

    @pl.when(i == nk - 1)
    def _():
        g = acc_g[...]
        active[...] = (g * jax.nn.sigmoid(g) * acc_u[...]).astype(active.dtype)

    @pl.when(i >= nk)
    def _():
        out_ref[...] = jnp.dot(active[...], down_ref[...], preferred_element_type=jnp.float32).astype(
            out_ref.dtype
        )


def expert_partial(inputs, gate_weight, up_weight, down_weight):
    slots, width = inputs.shape
    hidden = gate_weight.shape[1]
    tile = EXPERT_TILE
    nk, nn = width // tile, down_weight.shape[1] // tile
    k_of = lambda i: jnp.minimum(i, nk - 1)
    n_of = lambda i: jnp.maximum(i - nk, 0)
    return pl.pallas_call(
        lambda *refs: _expert_kernel(nk, *refs),
        grid=(nk + nn,),
        in_specs=[
            pl.BlockSpec((slots, tile), lambda i: (0, k_of(i))),
            pl.BlockSpec((tile, hidden), lambda i: (k_of(i), 0)),
            pl.BlockSpec((tile, hidden), lambda i: (k_of(i), 0)),
            pl.BlockSpec((hidden, tile), lambda i: (0, n_of(i))),
        ],
        out_specs=pl.BlockSpec((slots, tile), lambda i: (0, n_of(i))),
        out_shape=jax.ShapeDtypeStruct((slots, down_weight.shape[1]), jnp.bfloat16),
        scratch_shapes=[
            pltpu.VMEM((slots, hidden), jnp.float32),
            pltpu.VMEM((slots, hidden), jnp.float32),
            pltpu.VMEM((slots, hidden), jnp.bfloat16),
        ],
        compiler_params=pltpu.CompilerParams(
            dimension_semantics=("arbitrary",), vmem_limit_bytes=48 * 1024 * 1024
        ),
        cost_estimate=pl.CostEstimate(
            flops=6 * slots * width * hidden,
            transcendentals=slots * hidden,
            bytes_accessed=2 * (2 * slots * width + 3 * width * hidden),
        ),
    )(inputs, gate_weight, up_weight, down_weight)


def _lane_tile(col, width):
    return jnp.concatenate([col] * (width // LANES), axis=1) if width > LANES else col


def _end_kernel(step_ref, x_ref, decay_ref, b_ref, state_ref):
    steps, width = step_ref.shape
    rate = decay_ref[...]

    def body(k, state):
        base = pl.multiple_of(k * ROWS_PER_LOAD, ROWS_PER_LOAD)
        s_blk = step_ref[pl.ds(base, ROWS_PER_LOAD), :]
        x_blk = x_ref[pl.ds(base, ROWS_PER_LOAD), :].astype(jnp.float32)
        for i in range(ROWS_PER_LOAD):
            s_now = s_blk[i : i + 1]
            b_now = _lane_tile(b_ref[base + i], width)
            state = jnp.exp(-s_now * rate) * state + (s_now * x_blk[i : i + 1]) * b_now
        return state

    zero = jnp.zeros(rate.shape, jnp.float32)
    state_ref[...] = lax.fori_loop(0, steps // ROWS_PER_LOAD, body, zero)


def _out_kernel(state_in_ref, step_ref, x_ref, z_ref, decay_ref, b_ref, c_ref, skip_ref, gated_ref, y_ref):
    steps, width = step_ref.shape
    rate = decay_ref[...]
    skip = skip_ref[...]

    def body(k, state):
        base = pl.multiple_of(k * ROWS_PER_LOAD, ROWS_PER_LOAD)
        s_blk = step_ref[pl.ds(base, ROWS_PER_LOAD), :]
        x_blk = x_ref[pl.ds(base, ROWS_PER_LOAD), :].astype(jnp.float32)
        for i in range(ROWS_PER_LOAD):
            s_now = s_blk[i : i + 1]
            x_now = x_blk[i : i + 1]
            b_now = _lane_tile(b_ref[base + i], width)
            c_now = _lane_tile(c_ref[base + i], width)
            state = jnp.exp(-s_now * rate) * state + (s_now * x_now) * b_now
            y_ref[pl.ds(base + i, 1), :] = jnp.sum(c_now * state, axis=0, keepdims=True) + skip * x_now
        return state

    lax.fori_loop(0, steps // ROWS_PER_LOAD, body, state_in_ref[...])
    z = z_ref[...].astype(jnp.float32)
    gated_ref[...] = (y_ref[...] * (z * jax.nn.sigmoid(z))).astype(gated_ref.dtype)


def _columns(b_coef):
    rows = b_coef.astype(jnp.float32).T
    return jnp.broadcast_to(rows[:, :, None], rows.shape + (LANES,))


def scan_end(step_size, x_in, decay_rate, b_coef, width=512):
    steps, chans = step_size.shape
    states = decay_rate.shape[0]
    grid = (chans // width,)
    return pl.pallas_call(
        _end_kernel,
        grid=grid,
        in_specs=[
            pl.BlockSpec((steps, width), lambda j: (0, j)),
            pl.BlockSpec((steps, width), lambda j: (0, j)),
            pl.BlockSpec((states, width), lambda j: (0, j)),
            pl.BlockSpec((steps, states, LANES), lambda j: (0, 0, 0)),
        ],
        out_specs=pl.BlockSpec((states, width), lambda j: (0, j)),
        out_shape=jax.ShapeDtypeStruct((states, chans), jnp.float32),
        cost_estimate=pl.CostEstimate(
            flops=6 * steps * states * chans, transcendentals=steps * states * chans,
            bytes_accessed=steps * chans * 6 + states * chans * 8),
    )(step_size, x_in, decay_rate, _columns(b_coef))


def scan_gated(state_in, step_size, x_in, z_in, decay_rate, b_coef, c_coef, skip_gain, width=512):
    steps, chans = step_size.shape
    states = decay_rate.shape[0]
    grid = (chans // width,)
    col = lambda j: (0, j)
    return pl.pallas_call(
        _out_kernel,
        grid=grid,
        in_specs=[
            pl.BlockSpec((states, width), col),
            pl.BlockSpec((steps, width), col),
            pl.BlockSpec((steps, width), col),
            pl.BlockSpec((steps, width), col),
            pl.BlockSpec((states, width), col),
            pl.BlockSpec((steps, states, LANES), lambda j: (0, 0, 0)),
            pl.BlockSpec((steps, states, LANES), lambda j: (0, 0, 0)),
            pl.BlockSpec((1, width), col),
        ],
        out_specs=pl.BlockSpec((steps, width), col),
        out_shape=jax.ShapeDtypeStruct((steps, chans), jnp.bfloat16),
        scratch_shapes=[pltpu.VMEM((steps, width), jnp.float32)],
        cost_estimate=pl.CostEstimate(
            flops=9 * steps * states * chans, transcendentals=steps * states * chans + steps * chans,
            bytes_accessed=steps * chans * 10 + states * chans * 8),
    )(state_in, step_size, x_in, z_in, decay_rate, _columns(b_coef), _columns(c_coef), skip_gain[None, :])


def entering_state(state_end, step_total, decay_rate, axis):
    count, mine = (lax.axis_size(axis), lax.axis_index(axis))
    stacked = lax.all_gather(jnp.concatenate([state_end, step_total[None, :]], axis=0), axis)
    running = jnp.zeros_like(state_end)
    for position in range(count - 1):
        decay_then = jnp.exp(-decay_rate * stacked[position, -1][None, :])
        longer = decay_then * running + stacked[position, :-1]
        running = jnp.where(position < mine, longer, running)
    return running


def on_device(
    x_in,
    z_in,
    step_raw,
    step_bias,
    decay_rate,
    b_coef,
    c_coef,
    skip_gain,
    out_proj,
    residual,
    norm_gain,
    router_weight,
    expert_ids,
    gate_weight,
    up_weight,
    down_weight,
):
    step_size = jax.nn.softplus(step_raw.astype(jnp.float32) + step_bias[None, :])
    state_end = scan_end(step_size, x_in, decay_rate, b_coef)
    state_in = entering_state(state_end, jnp.sum(step_size, axis=0), decay_rate, "seq")
    gated = scan_gated(state_in, step_size, x_in, z_in, decay_rate, b_coef, c_coef, skip_gain)
    seq_count = lax.axis_size("seq")
    expert_count = lax.axis_size("expert")
    rows = residual.shape[0]
    gathered = lax.all_gather(gated, "seq", axis=0, tiled=True)
    column_part = jnp.dot(gathered, out_proj, preferred_element_type=jnp.float32).astype(jnp.bfloat16)
    column_part = column_part.reshape(seq_count * expert_count, rows, column_part.shape[1])
    swapped = lax.all_to_all(column_part, ("seq", "expert"), split_axis=0, concat_axis=0, tiled=True)
    swapped = swapped.reshape(seq_count, expert_count, rows, column_part.shape[2])
    summed = jnp.sum(swapped.astype(jnp.float32), axis=1)
    mamba_out = jnp.transpose(summed, (1, 0, 2)).reshape(rows, -1)
    hidden = (residual.astype(jnp.float32) + mamba_out).astype(jnp.bfloat16)
    hidden_f = hidden.astype(jnp.float32)
    width_d = hidden.shape[1]
    scale_cols = width_d // BLOCK
    normed = (
        hidden_f
        * lax.rsqrt(jnp.mean(hidden_f * hidden_f, axis=-1, keepdims=True) + 1e-05)
        * norm_gain[None, :]
    )
    blocked = normed.reshape(rows, scale_cols, BLOCK)
    scales = (jnp.max(jnp.abs(blocked), axis=-1) / 448.0 + 1e-06).astype(jnp.bfloat16)
    quant = (blocked / scales.astype(jnp.float32)[..., None]).astype(jnp.bfloat16)
    restored = (
        (quant.astype(jnp.float32) * scales.astype(jnp.float32)[..., None])
        .astype(jnp.bfloat16)
        .reshape(rows, width_d)
    )
    experts = router_weight.shape[1]
    probs = jax.nn.sigmoid(jnp.dot(restored, router_weight, preferred_element_type=jnp.float32))
    picks = expert_ids[:, :, None] == jnp.arange(experts, dtype=jnp.int32)[None, None, :]
    chosen = jnp.sum(jnp.where(picks, probs[:, None, :], jnp.float32(0.0)), axis=-1)
    weights = chosen / jnp.sum(chosen, axis=-1, keepdims=True)
    coef = jnp.sum(jnp.where(expert_ids == 0, weights, jnp.float32(0.0)), axis=1)
    wanted = jnp.any(expert_ids == 0, axis=1)
    wanted_int = wanted.astype(jnp.int32)
    slot_pos = jnp.cumsum(wanted_int) - wanted_int
    capacity = rows // 2
    table = (
        (slot_pos[None, :] == jnp.arange(capacity, dtype=jnp.int32)[:, None]) & wanted[None, :]
    ).astype(jnp.bfloat16)
    send_rows = jnp.dot(table, restored, preferred_element_type=jnp.float32).astype(jnp.bfloat16)
    inputs = lax.all_gather(send_rows, ("seq", "expert"), axis=0, tiled=True)
    own_sum = lax.psum_scatter(
        expert_partial(inputs, gate_weight, up_weight, down_weight),
        ("seq", "expert"),
        scatter_dimension=0,
        tiled=True,
    )
    returned = jnp.dot(table.T, own_sum, preferred_element_type=jnp.float32)
    return (hidden_f + coef[:, None] * returned).astype(jnp.bfloat16)


def solution(mesh):
    return jax.shard_map(
        on_device,
        mesh=mesh,
        in_specs=(
            P(("dp", "seq"), "expert"),
            P(("dp", "seq"), "expert"),
            P(("dp", "seq"), "expert"),
            P("expert"),
            P(None, "expert"),
            P(None, ("dp", "seq")),
            P(None, ("dp", "seq")),
            P("expert"),
            P("expert", "seq"),
            P(("dp", "seq", "expert"), None),
            P(),
            P(),
            P(("dp", "seq", "expert"), None),
            P(None, ("seq", "expert")),
            P(None, ("seq", "expert")),
            P(("seq", "expert"), None),
        ),
        out_specs=P(("dp", "seq", "expert"), None),
        check_vma=False,
    )
```

```python
import jax
import jax.numpy as jnp
from jax import lax
from jax.experimental import pallas as pl
from jax.experimental.pallas import tpu as pltpu
from jax.sharding import PartitionSpec as P

BLOCK = 128
LANES = 128
ROWS_PER_LOAD = 16

EXPERT_TILE = 2048


def _expert_kernel(nk, rows_ref, gate_ref, up_ref, down_ref, out_ref, acc_g, acc_u, active):
    i = pl.program_id(0)

    @pl.when(i == 0)
    def _():
        acc_g[...] = jnp.zeros_like(acc_g)
        acc_u[...] = jnp.zeros_like(acc_u)

    @pl.when(i < nk)
    def _():
        x = rows_ref[...]
        acc_g[...] += jnp.dot(x, gate_ref[...], preferred_element_type=jnp.float32)
        acc_u[...] += jnp.dot(x, up_ref[...], preferred_element_type=jnp.float32)

    @pl.when(i == nk - 1)
    def _():
        g = acc_g[...]
        active[...] = (g * jax.nn.sigmoid(g) * acc_u[...]).astype(active.dtype)

    @pl.when(i >= nk)
    def _():
        out_ref[...] = jnp.dot(active[...], down_ref[...], preferred_element_type=jnp.float32).astype(
            out_ref.dtype
        )


def expert_partial(inputs, gate_weight, up_weight, down_weight):
    slots, width = inputs.shape
    hidden = gate_weight.shape[1]
    tile = EXPERT_TILE
    nk, nn = width // tile, down_weight.shape[1] // tile
    k_of = lambda i: jnp.minimum(i, nk - 1)
    n_of = lambda i: jnp.maximum(i - nk, 0)
    return pl.pallas_call(
        lambda *refs: _expert_kernel(nk, *refs),
        grid=(nk + nn,),
        in_specs=[
            pl.BlockSpec((slots, tile), lambda i: (0, k_of(i))),
            pl.BlockSpec((tile, hidden), lambda i: (k_of(i), 0)),
            pl.BlockSpec((tile, hidden), lambda i: (k_of(i), 0)),
            pl.BlockSpec((hidden, tile), lambda i: (0, n_of(i))),
        ],
        out_specs=pl.BlockSpec((slots, tile), lambda i: (0, n_of(i))),
        out_shape=jax.ShapeDtypeStruct((slots, down_weight.shape[1]), jnp.bfloat16),
        scratch_shapes=[
            pltpu.VMEM((slots, hidden), jnp.float32),
            pltpu.VMEM((slots, hidden), jnp.float32),
            pltpu.VMEM((slots, hidden), jnp.bfloat16),
        ],
        compiler_params=pltpu.CompilerParams(
            dimension_semantics=("arbitrary",), vmem_limit_bytes=48 * 1024 * 1024
        ),
        cost_estimate=pl.CostEstimate(
            flops=6 * slots * width * hidden,
            transcendentals=slots * hidden,
            bytes_accessed=2 * (2 * slots * width + 3 * width * hidden),
        ),
    )(inputs, gate_weight, up_weight, down_weight)


def _lane_tile(col, width):
    return jnp.concatenate([col] * (width // LANES), axis=1) if width > LANES else col


def _end_kernel(step_ref, x_ref, decay_ref, b_ref, state_ref):
    steps, width = step_ref.shape
    states = decay_ref.shape[0]
    rate = decay_ref[...]

    def body(k, state):
        base = pl.multiple_of(k * ROWS_PER_LOAD, ROWS_PER_LOAD)
        s_blk = step_ref[pl.ds(base, ROWS_PER_LOAD), :]
        x_blk = x_ref[pl.ds(base, ROWS_PER_LOAD), :].astype(jnp.float32)
        for i in range(ROWS_PER_LOAD):
            s_now = s_blk[i : i + 1]
            b_now = _lane_tile(b_ref[base + i], width)
            state = jnp.exp(-s_now * rate) * state + (s_now * x_blk[i : i + 1]) * b_now
        return state

    zero = jnp.zeros(rate.shape, jnp.float32)
    state_ref[:states] = lax.fori_loop(0, steps // ROWS_PER_LOAD, body, zero)
    state_ref[states:] = jnp.sum(step_ref[...], axis=0, keepdims=True)


def _out_kernel(
    mine_ref, stacked_ref, step_ref, x_ref, z_ref, decay_ref, b_ref, c_ref, skip_ref, gated_ref, y_ref
):
    steps, width = step_ref.shape
    states = decay_ref.shape[0]
    rate = decay_ref[...]
    skip = skip_ref[...]
    mine = mine_ref[0]

    running = jnp.zeros(rate.shape, jnp.float32)
    for position in range(stacked_ref.shape[0] - 1):
        piece = stacked_ref[position]
        longer = jnp.exp(-rate * piece[states:]) * running + piece[:states]
        running = jnp.where(position < mine, longer, running)

    def body(k, state):
        base = pl.multiple_of(k * ROWS_PER_LOAD, ROWS_PER_LOAD)
        s_blk = step_ref[pl.ds(base, ROWS_PER_LOAD), :]
        x_blk = x_ref[pl.ds(base, ROWS_PER_LOAD), :].astype(jnp.float32)
        for i in range(ROWS_PER_LOAD):
            s_now = s_blk[i : i + 1]
            x_now = x_blk[i : i + 1]
            b_now = _lane_tile(b_ref[base + i], width)
            c_now = _lane_tile(c_ref[base + i], width)
            state = jnp.exp(-s_now * rate) * state + (s_now * x_now) * b_now
            y_ref[pl.ds(base + i, 1), :] = jnp.sum(c_now * state, axis=0, keepdims=True) + skip * x_now
        return state

    lax.fori_loop(0, steps // ROWS_PER_LOAD, body, running)
    z = z_ref[...].astype(jnp.float32)
    gated_ref[...] = (y_ref[...] * (z * jax.nn.sigmoid(z))).astype(gated_ref.dtype)


def _columns(b_coef, c_coef):
    rows = jnp.transpose(jnp.stack([b_coef, c_coef]).astype(jnp.float32), (0, 2, 1))
    return jnp.broadcast_to(rows[..., None], rows.shape + (LANES,))


def _coef_spec(steps, states, which):
    return pl.BlockSpec((None, steps, states, LANES), lambda j: (which, 0, 0, 0))


def scan_end(step_size, x_in, decay_rate, columns, width=512):
    steps, chans = step_size.shape
    states = decay_rate.shape[0]
    return pl.pallas_call(
        _end_kernel,
        grid=(chans // width,),
        in_specs=[
            pl.BlockSpec((steps, width), lambda j: (0, j)),
            pl.BlockSpec((steps, width), lambda j: (0, j)),
            pl.BlockSpec((states, width), lambda j: (0, j)),
            _coef_spec(steps, states, 0),
        ],
        out_specs=pl.BlockSpec((states + 1, width), lambda j: (0, j)),
        out_shape=jax.ShapeDtypeStruct((states + 1, chans), jnp.float32),
        cost_estimate=pl.CostEstimate(
            flops=6 * steps * states * chans, transcendentals=steps * states * chans,
            bytes_accessed=steps * chans * 6 + states * chans * 8),
    )(step_size, x_in, decay_rate, columns)


def scan_gated(mine, stacked, step_size, x_in, z_in, decay_rate, columns, skip_gain, width=512):
    steps, chans = step_size.shape
    states = decay_rate.shape[0]
    count = stacked.shape[0]
    col = lambda j: (0, j)
    return pl.pallas_call(
        _out_kernel,
        grid=(chans // width,),
        in_specs=[
            pl.BlockSpec(memory_space=pltpu.SMEM),
            pl.BlockSpec((count, states + 1, width), lambda j: (0, 0, j)),
            pl.BlockSpec((steps, width), col),
            pl.BlockSpec((steps, width), col),
            pl.BlockSpec((steps, width), col),
            pl.BlockSpec((states, width), col),
            _coef_spec(steps, states, 0),
            _coef_spec(steps, states, 1),
            pl.BlockSpec((1, width), col),
        ],
        out_specs=pl.BlockSpec((steps, width), col),
        out_shape=jax.ShapeDtypeStruct((steps, chans), jnp.bfloat16),
        scratch_shapes=[pltpu.VMEM((steps, width), jnp.float32)],
        cost_estimate=pl.CostEstimate(
            flops=9 * steps * states * chans, transcendentals=steps * states * chans + steps * chans,
            bytes_accessed=steps * chans * 10 + count * states * chans * 4),
    )(mine, stacked, step_size, x_in, z_in, decay_rate, columns, columns, skip_gain[None, :])


def on_device(
    x_in,
    z_in,
    step_raw,
    step_bias,
    decay_rate,
    b_coef,
    c_coef,
    skip_gain,
    out_proj,
    residual,
    norm_gain,
    router_weight,
    expert_ids,
    gate_weight,
    up_weight,
    down_weight,
):
    step_size = jax.nn.softplus(step_raw.astype(jnp.float32) + step_bias[None, :])
    columns = _columns(b_coef, c_coef)
    state_end = scan_end(step_size, x_in, decay_rate, columns)
    stacked = lax.all_gather(state_end, "seq")
    mine = lax.axis_index("seq").astype(jnp.int32).reshape(1)
    gated = scan_gated(mine, stacked, step_size, x_in, z_in, decay_rate, columns, skip_gain)
    seq_count = lax.axis_size("seq")
    expert_count = lax.axis_size("expert")
    rows = residual.shape[0]
    gathered = lax.all_gather(gated, "seq", axis=0, tiled=True)
    column_part = jnp.dot(gathered, out_proj, preferred_element_type=jnp.float32).astype(jnp.bfloat16)
    column_part = column_part.reshape(seq_count * expert_count, rows, column_part.shape[1])
    swapped = lax.all_to_all(column_part, ("seq", "expert"), split_axis=0, concat_axis=0, tiled=True)
    swapped = swapped.reshape(seq_count, expert_count, rows, column_part.shape[2])
    summed = jnp.sum(swapped.astype(jnp.float32), axis=1)
    mamba_out = jnp.transpose(summed, (1, 0, 2)).reshape(rows, -1)
    hidden = (residual.astype(jnp.float32) + mamba_out).astype(jnp.bfloat16)
    hidden_f = hidden.astype(jnp.float32)
    width_d = hidden.shape[1]
    scale_cols = width_d // BLOCK
    normed = (
        hidden_f
        * lax.rsqrt(jnp.mean(hidden_f * hidden_f, axis=-1, keepdims=True) + 1e-05)
        * norm_gain[None, :]
    )
    blocked = normed.reshape(rows, scale_cols, BLOCK)
    scales = (jnp.max(jnp.abs(blocked), axis=-1) / 448.0 + 1e-06).astype(jnp.bfloat16)
    quant = (blocked / scales.astype(jnp.float32)[..., None]).astype(jnp.bfloat16)
    restored = (
        (quant.astype(jnp.float32) * scales.astype(jnp.float32)[..., None])
        .astype(jnp.bfloat16)
        .reshape(rows, width_d)
    )
    experts = router_weight.shape[1]
    probs = jax.nn.sigmoid(jnp.dot(restored, router_weight, preferred_element_type=jnp.float32))
    picks = expert_ids[:, :, None] == jnp.arange(experts, dtype=jnp.int32)[None, None, :]
    chosen = jnp.sum(jnp.where(picks, probs[:, None, :], jnp.float32(0.0)), axis=-1)
    weights = chosen / jnp.sum(chosen, axis=-1, keepdims=True)
    coef = jnp.sum(jnp.where(expert_ids == 0, weights, jnp.float32(0.0)), axis=1)
    wanted = jnp.any(expert_ids == 0, axis=1)
    wanted_int = wanted.astype(jnp.int32)
    slot_pos = jnp.cumsum(wanted_int) - wanted_int
    capacity = rows // 2
    table = (
        (slot_pos[None, :] == jnp.arange(capacity, dtype=jnp.int32)[:, None]) & wanted[None, :]
    ).astype(jnp.bfloat16)
    send_rows = jnp.dot(table, restored, preferred_element_type=jnp.float32).astype(jnp.bfloat16)
    inputs = lax.all_gather(send_rows, ("seq", "expert"), axis=0, tiled=True)
    own_sum = lax.psum_scatter(
        expert_partial(inputs, gate_weight, up_weight, down_weight),
        ("seq", "expert"),
        scatter_dimension=0,
        tiled=True,
    )
    returned = jnp.dot(table.T, own_sum, preferred_element_type=jnp.float32)
    return (hidden_f + coef[:, None] * returned).astype(jnp.bfloat16)


def solution(mesh):
    return jax.shard_map(
        on_device,
        mesh=mesh,
        in_specs=(
            P(("dp", "seq"), "expert"),
            P(("dp", "seq"), "expert"),
            P(("dp", "seq"), "expert"),
            P("expert"),
            P(None, "expert"),
            P(None, ("dp", "seq")),
            P(None, ("dp", "seq")),
            P("expert"),
            P("expert", "seq"),
            P(("dp", "seq", "expert"), None),
            P(),
            P(),
            P(("dp", "seq", "expert"), None),
            P(None, ("seq", "expert")),
            P(None, ("seq", "expert")),
            P(("seq", "expert"), None),
        ),
        out_specs=P(("dp", "seq", "expert"), None),
        check_vma=False,
    )
```

```python
import jax
import jax.numpy as jnp
from jax import lax
from jax.experimental import pallas as pl
from jax.experimental.pallas import tpu as pltpu
from jax.sharding import PartitionSpec as P

BLOCK = 128
LANES = 128
ROWS_PER_LOAD = 16

EXPERT_TILE = 2048


def _expert_kernel(nk, rows_ref, gate_ref, up_ref, down_ref, out_ref, acc_g, acc_u, active):
    i = pl.program_id(0)

    @pl.when(i == 0)
    def _():
        acc_g[...] = jnp.zeros_like(acc_g)
        acc_u[...] = jnp.zeros_like(acc_u)

    @pl.when(i < nk)
    def _():
        x = rows_ref[...]
        acc_g[...] += jnp.dot(x, gate_ref[...], preferred_element_type=jnp.float32)
        acc_u[...] += jnp.dot(x, up_ref[...], preferred_element_type=jnp.float32)

    @pl.when(i == nk - 1)
    def _():
        g = acc_g[...]
        active[...] = (g * jax.nn.sigmoid(g) * acc_u[...]).astype(active.dtype)

    @pl.when(i >= nk)
    def _():
        out_ref[...] = jnp.dot(active[...], down_ref[...], preferred_element_type=jnp.float32).astype(
            out_ref.dtype
        )


def expert_partial(inputs, gate_weight, up_weight, down_weight):
    slots, width = inputs.shape
    hidden = gate_weight.shape[1]
    tile = EXPERT_TILE
    nk, nn = width // tile, down_weight.shape[1] // tile
    k_of = lambda i: jnp.minimum(i, nk - 1)
    n_of = lambda i: jnp.maximum(i - nk, 0)
    return pl.pallas_call(
        lambda *refs: _expert_kernel(nk, *refs),
        grid=(nk + nn,),
        in_specs=[
            pl.BlockSpec((slots, tile), lambda i: (0, k_of(i))),
            pl.BlockSpec((tile, hidden), lambda i: (k_of(i), 0)),
            pl.BlockSpec((tile, hidden), lambda i: (k_of(i), 0)),
            pl.BlockSpec((hidden, tile), lambda i: (0, n_of(i))),
        ],
        out_specs=pl.BlockSpec((slots, tile), lambda i: (0, n_of(i))),
        out_shape=jax.ShapeDtypeStruct((slots, down_weight.shape[1]), jnp.bfloat16),
        scratch_shapes=[
            pltpu.VMEM((slots, hidden), jnp.float32),
            pltpu.VMEM((slots, hidden), jnp.float32),
            pltpu.VMEM((slots, hidden), jnp.bfloat16),
        ],
        compiler_params=pltpu.CompilerParams(
            dimension_semantics=("arbitrary",), vmem_limit_bytes=48 * 1024 * 1024
        ),
        cost_estimate=pl.CostEstimate(
            flops=6 * slots * width * hidden,
            transcendentals=slots * hidden,
            bytes_accessed=2 * (2 * slots * width + 3 * width * hidden),
        ),
    )(inputs, gate_weight, up_weight, down_weight)


def _lane_tile(col, width):
    return jnp.concatenate([col] * (width // LANES), axis=1) if width > LANES else col


def _step_rows(raw_ref, bias_ref, base):
    raw = raw_ref[pl.ds(base, ROWS_PER_LOAD), :].astype(jnp.float32)
    return jax.nn.softplus(raw + bias_ref[...])


def _end_kernel(raw_ref, bias_ref, x_ref, decay_ref, b_ref, state_ref):
    steps, width = raw_ref.shape
    states = decay_ref.shape[0]
    rate = decay_ref[...]

    def body(k, carry):
        state, total = carry
        base = pl.multiple_of(k * ROWS_PER_LOAD, ROWS_PER_LOAD)
        s_blk = _step_rows(raw_ref, bias_ref, base)
        x_blk = x_ref[pl.ds(base, ROWS_PER_LOAD), :].astype(jnp.float32)
        for i in range(ROWS_PER_LOAD):
            s_now = s_blk[i : i + 1]
            b_now = _lane_tile(b_ref[base + i], width)
            state = jnp.exp(-s_now * rate) * state + (s_now * x_blk[i : i + 1]) * b_now
        return state, total + jnp.sum(s_blk, axis=0, keepdims=True)

    zero = (jnp.zeros(rate.shape, jnp.float32), jnp.zeros((1, width), jnp.float32))
    state, total = lax.fori_loop(0, steps // ROWS_PER_LOAD, body, zero)
    state_ref[:states] = state
    state_ref[states:] = total


def _out_kernel(
    mine_ref, stacked_ref, raw_ref, bias_ref, x_ref, z_ref, decay_ref, b_ref, c_ref, skip_ref, gated_ref, y_ref
):
    steps, width = raw_ref.shape
    states = decay_ref.shape[0]
    rate = decay_ref[...]
    skip = skip_ref[...]
    mine = mine_ref[0]

    running = jnp.zeros(rate.shape, jnp.float32)
    for position in range(stacked_ref.shape[0] - 1):
        piece = stacked_ref[position]
        longer = jnp.exp(-rate * piece[states:]) * running + piece[:states]
        running = jnp.where(position < mine, longer, running)

    def body(k, state):
        base = pl.multiple_of(k * ROWS_PER_LOAD, ROWS_PER_LOAD)
        s_blk = _step_rows(raw_ref, bias_ref, base)
        x_blk = x_ref[pl.ds(base, ROWS_PER_LOAD), :].astype(jnp.float32)
        for i in range(ROWS_PER_LOAD):
            s_now = s_blk[i : i + 1]
            x_now = x_blk[i : i + 1]
            b_now = _lane_tile(b_ref[base + i], width)
            c_now = _lane_tile(c_ref[base + i], width)
            state = jnp.exp(-s_now * rate) * state + (s_now * x_now) * b_now
            y_ref[pl.ds(base + i, 1), :] = jnp.sum(c_now * state, axis=0, keepdims=True) + skip * x_now
        return state

    lax.fori_loop(0, steps // ROWS_PER_LOAD, body, running)
    z = z_ref[...].astype(jnp.float32)
    gated_ref[...] = (y_ref[...] * (z * jax.nn.sigmoid(z))).astype(gated_ref.dtype)


def _columns(b_coef, c_coef):
    rows = jnp.transpose(jnp.stack([b_coef, c_coef]).astype(jnp.float32), (0, 2, 1))
    return jnp.broadcast_to(rows[..., None], rows.shape + (LANES,))


def _coef_spec(steps, states, which):
    return pl.BlockSpec((None, steps, states, LANES), lambda j: (which, 0, 0, 0))


def scan_end(step_raw, step_bias, x_in, decay_rate, columns, width=512):
    steps, chans = step_raw.shape
    states = decay_rate.shape[0]
    return pl.pallas_call(
        _end_kernel,
        grid=(chans // width,),
        in_specs=[
            pl.BlockSpec((steps, width), lambda j: (0, j)),
            pl.BlockSpec((1, width), lambda j: (0, j)),
            pl.BlockSpec((steps, width), lambda j: (0, j)),
            pl.BlockSpec((states, width), lambda j: (0, j)),
            _coef_spec(steps, states, 0),
        ],
        out_specs=pl.BlockSpec((states + 1, width), lambda j: (0, j)),
        out_shape=jax.ShapeDtypeStruct((states + 1, chans), jnp.float32),
        cost_estimate=pl.CostEstimate(
            flops=6 * steps * states * chans, transcendentals=steps * states * chans,
            bytes_accessed=steps * chans * 6 + states * chans * 8),
    )(step_raw, step_bias[None, :], x_in, decay_rate, columns)


def scan_gated(mine, stacked, step_raw, step_bias, x_in, z_in, decay_rate, columns, skip_gain, width=512):
    steps, chans = step_raw.shape
    states = decay_rate.shape[0]
    count = stacked.shape[0]
    col = lambda j: (0, j)
    return pl.pallas_call(
        _out_kernel,
        grid=(chans // width,),
        in_specs=[
            pl.BlockSpec(memory_space=pltpu.SMEM),
            pl.BlockSpec((count, states + 1, width), lambda j: (0, 0, j)),
            pl.BlockSpec((steps, width), col),
            pl.BlockSpec((1, width), col),
            pl.BlockSpec((steps, width), col),
            pl.BlockSpec((steps, width), col),
            pl.BlockSpec((states, width), col),
            _coef_spec(steps, states, 0),
            _coef_spec(steps, states, 1),
            pl.BlockSpec((1, width), col),
        ],
        out_specs=pl.BlockSpec((steps, width), col),
        out_shape=jax.ShapeDtypeStruct((steps, chans), jnp.bfloat16),
        scratch_shapes=[pltpu.VMEM((steps, width), jnp.float32)],
        cost_estimate=pl.CostEstimate(
            flops=9 * steps * states * chans, transcendentals=steps * states * chans + steps * chans,
            bytes_accessed=steps * chans * 10 + count * states * chans * 4),
    )(mine, stacked, step_raw, step_bias[None, :], x_in, z_in, decay_rate, columns, columns, skip_gain[None, :])


def on_device(
    x_in,
    z_in,
    step_raw,
    step_bias,
    decay_rate,
    b_coef,
    c_coef,
    skip_gain,
    out_proj,
    residual,
    norm_gain,
    router_weight,
    expert_ids,
    gate_weight,
    up_weight,
    down_weight,
):
    columns = _columns(b_coef, c_coef)
    state_end = scan_end(step_raw, step_bias, x_in, decay_rate, columns)
    stacked = lax.all_gather(state_end, "seq")
    mine = lax.axis_index("seq").astype(jnp.int32).reshape(1)
    gated = scan_gated(mine, stacked, step_raw, step_bias, x_in, z_in, decay_rate, columns, skip_gain)
    seq_count = lax.axis_size("seq")
    expert_count = lax.axis_size("expert")
    rows = residual.shape[0]
    gathered = lax.all_gather(gated, "seq", axis=0, tiled=True)
    column_part = jnp.dot(gathered, out_proj, preferred_element_type=jnp.float32).astype(jnp.bfloat16)
    column_part = column_part.reshape(seq_count * expert_count, rows, column_part.shape[1])
    swapped = lax.all_to_all(column_part, ("seq", "expert"), split_axis=0, concat_axis=0, tiled=True)
    swapped = swapped.reshape(seq_count, expert_count, rows, column_part.shape[2])
    summed = jnp.sum(swapped.astype(jnp.float32), axis=1)
    mamba_out = jnp.transpose(summed, (1, 0, 2)).reshape(rows, -1)
    hidden = (residual.astype(jnp.float32) + mamba_out).astype(jnp.bfloat16)
    hidden_f = hidden.astype(jnp.float32)
    width_d = hidden.shape[1]
    scale_cols = width_d // BLOCK
    normed = (
        hidden_f
        * lax.rsqrt(jnp.mean(hidden_f * hidden_f, axis=-1, keepdims=True) + 1e-05)
        * norm_gain[None, :]
    )
    blocked = normed.reshape(rows, scale_cols, BLOCK)
    scales = (jnp.max(jnp.abs(blocked), axis=-1) / 448.0 + 1e-06).astype(jnp.bfloat16)
    quant = (blocked / scales.astype(jnp.float32)[..., None]).astype(jnp.bfloat16)
    restored = (
        (quant.astype(jnp.float32) * scales.astype(jnp.float32)[..., None])
        .astype(jnp.bfloat16)
        .reshape(rows, width_d)
    )
    experts = router_weight.shape[1]
    probs = jax.nn.sigmoid(jnp.dot(restored, router_weight, preferred_element_type=jnp.float32))
    picks = expert_ids[:, :, None] == jnp.arange(experts, dtype=jnp.int32)[None, None, :]
    chosen = jnp.sum(jnp.where(picks, probs[:, None, :], jnp.float32(0.0)), axis=-1)
    weights = chosen / jnp.sum(chosen, axis=-1, keepdims=True)
    coef = jnp.sum(jnp.where(expert_ids == 0, weights, jnp.float32(0.0)), axis=1)
    wanted = jnp.any(expert_ids == 0, axis=1)
    wanted_int = wanted.astype(jnp.int32)
    slot_pos = jnp.cumsum(wanted_int) - wanted_int
    capacity = rows // 2
    table = (
        (slot_pos[None, :] == jnp.arange(capacity, dtype=jnp.int32)[:, None]) & wanted[None, :]
    ).astype(jnp.bfloat16)
    send_rows = jnp.dot(table, restored, preferred_element_type=jnp.float32).astype(jnp.bfloat16)
    inputs = lax.all_gather(send_rows, ("seq", "expert"), axis=0, tiled=True)
    own_sum = lax.psum_scatter(
        expert_partial(inputs, gate_weight, up_weight, down_weight),
        ("seq", "expert"),
        scatter_dimension=0,
        tiled=True,
    )
    returned = jnp.dot(table.T, own_sum, preferred_element_type=jnp.float32)
    return (hidden_f + coef[:, None] * returned).astype(jnp.bfloat16)


def solution(mesh):
    return jax.shard_map(
        on_device,
        mesh=mesh,
        in_specs=(
            P(("dp", "seq"), "expert"),
            P(("dp", "seq"), "expert"),
            P(("dp", "seq"), "expert"),
            P("expert"),
            P(None, "expert"),
            P(None, ("dp", "seq")),
            P(None, ("dp", "seq")),
            P("expert"),
            P("expert", "seq"),
            P(("dp", "seq", "expert"), None),
            P(),
            P(),
            P(("dp", "seq", "expert"), None),
            P(None, ("seq", "expert")),
            P(None, ("seq", "expert")),
            P(("seq", "expert"), None),
        ),
        out_specs=P(("dp", "seq", "expert"), None),
        check_vma=False,
    )
```

```python
import jax
import jax.numpy as jnp
from jax import lax
from jax.experimental import pallas as pl
from jax.experimental.pallas import tpu as pltpu
from jax.sharding import PartitionSpec as P

BLOCK = 128
LANES = 128
ROWS_PER_LOAD = 16

EXPERT_TILE = 2048


def _expert_kernel(nk, rows_ref, gate_ref, up_ref, down_ref, out_ref, acc_g, acc_u, active):
    i = pl.program_id(0)

    @pl.when(i == 0)
    def _():
        acc_g[...] = jnp.zeros_like(acc_g)
        acc_u[...] = jnp.zeros_like(acc_u)

    @pl.when(i < nk)
    def _():
        x = rows_ref[...]
        acc_g[...] += jnp.dot(x, gate_ref[...], preferred_element_type=jnp.float32)
        acc_u[...] += jnp.dot(x, up_ref[...], preferred_element_type=jnp.float32)

    @pl.when(i == nk - 1)
    def _():
        g = acc_g[...]
        active[...] = (g * jax.nn.sigmoid(g) * acc_u[...]).astype(active.dtype)

    @pl.when(i >= nk)
    def _():
        out_ref[...] = jnp.dot(active[...], down_ref[...], preferred_element_type=jnp.float32).astype(
            out_ref.dtype
        )


def expert_partial(inputs, gate_weight, up_weight, down_weight):
    slots, width = inputs.shape
    hidden = gate_weight.shape[1]
    tile = EXPERT_TILE
    nk, nn = width // tile, down_weight.shape[1] // tile
    k_of = lambda i: jnp.minimum(i, nk - 1)
    n_of = lambda i: jnp.maximum(i - nk, 0)
    return pl.pallas_call(
        lambda *refs: _expert_kernel(nk, *refs),
        grid=(nk + nn,),
        in_specs=[
            pl.BlockSpec((slots, tile), lambda i: (0, k_of(i))),
            pl.BlockSpec((tile, hidden), lambda i: (k_of(i), 0)),
            pl.BlockSpec((tile, hidden), lambda i: (k_of(i), 0)),
            pl.BlockSpec((hidden, tile), lambda i: (0, n_of(i))),
        ],
        out_specs=pl.BlockSpec((slots, tile), lambda i: (0, n_of(i))),
        out_shape=jax.ShapeDtypeStruct((slots, down_weight.shape[1]), jnp.bfloat16),
        scratch_shapes=[
            pltpu.VMEM((slots, hidden), jnp.float32),
            pltpu.VMEM((slots, hidden), jnp.float32),
            pltpu.VMEM((slots, hidden), jnp.bfloat16),
        ],
        compiler_params=pltpu.CompilerParams(
            dimension_semantics=("arbitrary",), vmem_limit_bytes=48 * 1024 * 1024
        ),
        cost_estimate=pl.CostEstimate(
            flops=6 * slots * width * hidden,
            transcendentals=slots * hidden,
            bytes_accessed=2 * (2 * slots * width + 3 * width * hidden),
        ),
    )(inputs, gate_weight, up_weight, down_weight)


def _project_kernel(x_ref, w_ref, out_ref):
    out_ref[...] = jnp.dot(x_ref[...], w_ref[...], preferred_element_type=jnp.float32).astype(
        out_ref.dtype
    )


def project(gathered, out_proj, tile=512):
    rows, inner = gathered.shape
    cols = out_proj.shape[1]
    return pl.pallas_call(
        _project_kernel,
        grid=(rows // tile, cols // tile),
        in_specs=[
            pl.BlockSpec((tile, inner), lambda i, j: (i, 0)),
            pl.BlockSpec((inner, tile), lambda i, j: (0, j)),
        ],
        out_specs=pl.BlockSpec((tile, tile), lambda i, j: (i, j)),
        out_shape=jax.ShapeDtypeStruct((rows, cols), jnp.bfloat16),
        compiler_params=pltpu.CompilerParams(dimension_semantics=("arbitrary", "arbitrary")),
        cost_estimate=pl.CostEstimate(
            flops=2 * rows * inner * cols, transcendentals=0,
            bytes_accessed=2 * (rows * inner + inner * cols + rows * cols)),
    )(gathered, out_proj)


def _lane_tile(col, width):
    return jnp.concatenate([col] * (width // LANES), axis=1) if width > LANES else col


def _step_rows(raw_ref, bias_ref, base):
    raw = raw_ref[pl.ds(base, ROWS_PER_LOAD), :].astype(jnp.float32)
    return jax.nn.softplus(raw + bias_ref[...])


def _end_kernel(raw_ref, bias_ref, x_ref, decay_ref, b_ref, state_ref):
    steps, width = raw_ref.shape
    states = decay_ref.shape[0]
    rate = decay_ref[...]

    def body(k, carry):
        state, total = carry
        base = pl.multiple_of(k * ROWS_PER_LOAD, ROWS_PER_LOAD)
        s_blk = _step_rows(raw_ref, bias_ref, base)
        x_blk = x_ref[pl.ds(base, ROWS_PER_LOAD), :].astype(jnp.float32)
        for i in range(ROWS_PER_LOAD):
            s_now = s_blk[i : i + 1]
            b_now = _lane_tile(b_ref[base + i], width)
            state = jnp.exp(-s_now * rate) * state + (s_now * x_blk[i : i + 1]) * b_now
        return state, total + jnp.sum(s_blk, axis=0, keepdims=True)

    zero = (jnp.zeros(rate.shape, jnp.float32), jnp.zeros((1, width), jnp.float32))
    state, total = lax.fori_loop(0, steps // ROWS_PER_LOAD, body, zero)
    state_ref[:states] = state
    state_ref[states:] = total


def _out_kernel(
    mine_ref, stacked_ref, raw_ref, bias_ref, x_ref, z_ref, decay_ref, b_ref, c_ref, skip_ref, gated_ref, y_ref
):
    steps, width = raw_ref.shape
    states = decay_ref.shape[0]
    rate = decay_ref[...]
    skip = skip_ref[...]
    mine = mine_ref[0]

    running = jnp.zeros(rate.shape, jnp.float32)
    for position in range(stacked_ref.shape[0] - 1):
        piece = stacked_ref[position]
        longer = jnp.exp(-rate * piece[states:]) * running + piece[:states]
        running = jnp.where(position < mine, longer, running)

    def body(k, state):
        base = pl.multiple_of(k * ROWS_PER_LOAD, ROWS_PER_LOAD)
        s_blk = _step_rows(raw_ref, bias_ref, base)
        x_blk = x_ref[pl.ds(base, ROWS_PER_LOAD), :].astype(jnp.float32)
        for i in range(ROWS_PER_LOAD):
            s_now = s_blk[i : i + 1]
            x_now = x_blk[i : i + 1]
            b_now = _lane_tile(b_ref[base + i], width)
            c_now = _lane_tile(c_ref[base + i], width)
            state = jnp.exp(-s_now * rate) * state + (s_now * x_now) * b_now
            y_ref[pl.ds(base + i, 1), :] = jnp.sum(c_now * state, axis=0, keepdims=True) + skip * x_now
        return state

    lax.fori_loop(0, steps // ROWS_PER_LOAD, body, running)
    z = z_ref[...].astype(jnp.float32)
    gated_ref[...] = (y_ref[...] * (z * jax.nn.sigmoid(z))).astype(gated_ref.dtype)


def _columns(b_coef, c_coef):
    rows = jnp.transpose(jnp.stack([b_coef, c_coef]).astype(jnp.float32), (0, 2, 1))
    return jnp.broadcast_to(rows[..., None], rows.shape + (LANES,))


def _coef_spec(steps, states, which):
    return pl.BlockSpec((None, steps, states, LANES), lambda j: (which, 0, 0, 0))


def scan_end(step_raw, step_bias, x_in, decay_rate, columns, width=512):
    steps, chans = step_raw.shape
    states = decay_rate.shape[0]
    return pl.pallas_call(
        _end_kernel,
        grid=(chans // width,),
        in_specs=[
            pl.BlockSpec((steps, width), lambda j: (0, j)),
            pl.BlockSpec((1, width), lambda j: (0, j)),
            pl.BlockSpec((steps, width), lambda j: (0, j)),
            pl.BlockSpec((states, width), lambda j: (0, j)),
            _coef_spec(steps, states, 0),
        ],
        out_specs=pl.BlockSpec((states + 1, width), lambda j: (0, j)),
        out_shape=jax.ShapeDtypeStruct((states + 1, chans), jnp.float32),
        cost_estimate=pl.CostEstimate(
            flops=6 * steps * states * chans, transcendentals=steps * states * chans,
            bytes_accessed=steps * chans * 6 + states * chans * 8),
    )(step_raw, step_bias[None, :], x_in, decay_rate, columns)


def scan_gated(mine, stacked, step_raw, step_bias, x_in, z_in, decay_rate, columns, skip_gain, width=512):
    steps, chans = step_raw.shape
    states = decay_rate.shape[0]
    count = stacked.shape[0]
    col = lambda j: (0, j)
    return pl.pallas_call(
        _out_kernel,
        grid=(chans // width,),
        in_specs=[
            pl.BlockSpec(memory_space=pltpu.SMEM),
            pl.BlockSpec((count, states + 1, width), lambda j: (0, 0, j)),
            pl.BlockSpec((steps, width), col),
            pl.BlockSpec((1, width), col),
            pl.BlockSpec((steps, width), col),
            pl.BlockSpec((steps, width), col),
            pl.BlockSpec((states, width), col),
            _coef_spec(steps, states, 0),
            _coef_spec(steps, states, 1),
            pl.BlockSpec((1, width), col),
        ],
        out_specs=pl.BlockSpec((steps, width), col),
        out_shape=jax.ShapeDtypeStruct((steps, chans), jnp.bfloat16),
        scratch_shapes=[pltpu.VMEM((steps, width), jnp.float32)],
        cost_estimate=pl.CostEstimate(
            flops=9 * steps * states * chans, transcendentals=steps * states * chans + steps * chans,
            bytes_accessed=steps * chans * 10 + count * states * chans * 4),
    )(mine, stacked, step_raw, step_bias[None, :], x_in, z_in, decay_rate, columns, columns, skip_gain[None, :])


def on_device(
    x_in,
    z_in,
    step_raw,
    step_bias,
    decay_rate,
    b_coef,
    c_coef,
    skip_gain,
    out_proj,
    residual,
    norm_gain,
    router_weight,
    expert_ids,
    gate_weight,
    up_weight,
    down_weight,
):
    columns = _columns(b_coef, c_coef)
    state_end = scan_end(step_raw, step_bias, x_in, decay_rate, columns)
    stacked = lax.all_gather(state_end, "seq")
    mine = lax.axis_index("seq").astype(jnp.int32).reshape(1)
    gated = scan_gated(mine, stacked, step_raw, step_bias, x_in, z_in, decay_rate, columns, skip_gain)
    seq_count = lax.axis_size("seq")
    expert_count = lax.axis_size("expert")
    rows = residual.shape[0]
    gathered = lax.all_gather(gated, "seq", axis=0, tiled=True)
    column_part = project(gathered, out_proj)
    column_part = column_part.reshape(seq_count * expert_count, rows, column_part.shape[1])
    swapped = lax.all_to_all(column_part, ("seq", "expert"), split_axis=0, concat_axis=0, tiled=True)
    swapped = swapped.reshape(seq_count, expert_count, rows, column_part.shape[2])
    summed = jnp.sum(swapped.astype(jnp.float32), axis=1)
    mamba_out = jnp.transpose(summed, (1, 0, 2)).reshape(rows, -1)
    hidden = (residual.astype(jnp.float32) + mamba_out).astype(jnp.bfloat16)
    hidden_f = hidden.astype(jnp.float32)
    width_d = hidden.shape[1]
    scale_cols = width_d // BLOCK
    normed = (
        hidden_f
        * lax.rsqrt(jnp.mean(hidden_f * hidden_f, axis=-1, keepdims=True) + 1e-05)
        * norm_gain[None, :]
    )
    blocked = normed.reshape(rows, scale_cols, BLOCK)
    scales = (jnp.max(jnp.abs(blocked), axis=-1) / 448.0 + 1e-06).astype(jnp.bfloat16)
    quant = (blocked / scales.astype(jnp.float32)[..., None]).astype(jnp.bfloat16)
    restored = (
        (quant.astype(jnp.float32) * scales.astype(jnp.float32)[..., None])
        .astype(jnp.bfloat16)
        .reshape(rows, width_d)
    )
    experts = router_weight.shape[1]
    probs = jax.nn.sigmoid(jnp.dot(restored, router_weight, preferred_element_type=jnp.float32))
    picks = expert_ids[:, :, None] == jnp.arange(experts, dtype=jnp.int32)[None, None, :]
    chosen = jnp.sum(jnp.where(picks, probs[:, None, :], jnp.float32(0.0)), axis=-1)
    weights = chosen / jnp.sum(chosen, axis=-1, keepdims=True)
    coef = jnp.sum(jnp.where(expert_ids == 0, weights, jnp.float32(0.0)), axis=1)
    wanted = jnp.any(expert_ids == 0, axis=1)
    wanted_int = wanted.astype(jnp.int32)
    slot_pos = jnp.cumsum(wanted_int) - wanted_int
    capacity = rows // 2
    table = (
        (slot_pos[None, :] == jnp.arange(capacity, dtype=jnp.int32)[:, None]) & wanted[None, :]
    ).astype(jnp.bfloat16)
    send_rows = jnp.dot(table, restored, preferred_element_type=jnp.float32).astype(jnp.bfloat16)
    inputs = lax.all_gather(send_rows, ("seq", "expert"), axis=0, tiled=True)
    own_sum = lax.psum_scatter(
        expert_partial(inputs, gate_weight, up_weight, down_weight),
        ("seq", "expert"),
        scatter_dimension=0,
        tiled=True,
    )
    returned = jnp.dot(table.T, own_sum, preferred_element_type=jnp.float32)
    return (hidden_f + coef[:, None] * returned).astype(jnp.bfloat16)


def solution(mesh):
    return jax.shard_map(
        on_device,
        mesh=mesh,
        in_specs=(
            P(("dp", "seq"), "expert"),
            P(("dp", "seq"), "expert"),
            P(("dp", "seq"), "expert"),
            P("expert"),
            P(None, "expert"),
            P(None, ("dp", "seq")),
            P(None, ("dp", "seq")),
            P("expert"),
            P("expert", "seq"),
            P(("dp", "seq", "expert"), None),
            P(),
            P(),
            P(("dp", "seq", "expert"), None),
            P(None, ("seq", "expert")),
            P(None, ("seq", "expert")),
            P(("seq", "expert"), None),
        ),
        out_specs=P(("dp", "seq", "expert"), None),
        check_vma=False,
    )
```

```python
import jax
import jax.numpy as jnp
from jax import lax
from jax.experimental import pallas as pl
from jax.experimental.pallas import tpu as pltpu
from jax.sharding import PartitionSpec as P

BLOCK = 128
LANES = 128
ROWS_PER_LOAD = 16

EXPERT_TILE = 2048


def _expert_kernel(nk, rows_ref, gate_ref, up_ref, down_ref, out_ref, acc_g, acc_u, active):
    i = pl.program_id(0)

    @pl.when(i == 0)
    def _():
        acc_g[...] = jnp.zeros_like(acc_g)
        acc_u[...] = jnp.zeros_like(acc_u)

    @pl.when(i < nk)
    def _():
        x = rows_ref[...]
        acc_g[...] += jnp.dot(x, gate_ref[...], preferred_element_type=jnp.float32)
        acc_u[...] += jnp.dot(x, up_ref[...], preferred_element_type=jnp.float32)

    @pl.when(i == nk - 1)
    def _():
        g = acc_g[...]
        active[...] = (g * jax.nn.sigmoid(g) * acc_u[...]).astype(active.dtype)

    @pl.when(i >= nk)
    def _():
        out_ref[...] = jnp.dot(active[...], down_ref[...], preferred_element_type=jnp.float32).astype(
            out_ref.dtype
        )


def expert_partial(inputs, gate_weight, up_weight, down_weight):
    slots, width = inputs.shape
    hidden = gate_weight.shape[1]
    tile = EXPERT_TILE
    nk, nn = width // tile, down_weight.shape[1] // tile
    k_of = lambda i: jnp.minimum(i, nk - 1)
    n_of = lambda i: jnp.maximum(i - nk, 0)
    return pl.pallas_call(
        lambda *refs: _expert_kernel(nk, *refs),
        grid=(nk + nn,),
        in_specs=[
            pl.BlockSpec((slots, tile), lambda i: (0, k_of(i))),
            pl.BlockSpec((tile, hidden), lambda i: (k_of(i), 0)),
            pl.BlockSpec((tile, hidden), lambda i: (k_of(i), 0)),
            pl.BlockSpec((hidden, tile), lambda i: (0, n_of(i))),
        ],
        out_specs=pl.BlockSpec((slots, tile), lambda i: (0, n_of(i))),
        out_shape=jax.ShapeDtypeStruct((slots, down_weight.shape[1]), jnp.bfloat16),
        scratch_shapes=[
            pltpu.VMEM((slots, hidden), jnp.float32),
            pltpu.VMEM((slots, hidden), jnp.float32),
            pltpu.VMEM((slots, hidden), jnp.bfloat16),
        ],
        compiler_params=pltpu.CompilerParams(
            dimension_semantics=("arbitrary",), vmem_limit_bytes=48 * 1024 * 1024
        ),
        cost_estimate=pl.CostEstimate(
            flops=6 * slots * width * hidden,
            transcendentals=slots * hidden,
            bytes_accessed=2 * (2 * slots * width + 3 * width * hidden),
        ),
    )(inputs, gate_weight, up_weight, down_weight)


def _lane_tile(col, width):
    return jnp.concatenate([col] * (width // LANES), axis=1) if width > LANES else col


def _step_rows(raw_ref, bias_ref, base):
    raw = raw_ref[pl.ds(base, ROWS_PER_LOAD), :].astype(jnp.float32)
    return jax.nn.softplus(raw + bias_ref[...])


def _end_kernel(raw_ref, bias_ref, x_ref, decay_ref, b_ref, state_ref):
    steps, width = raw_ref.shape
    states = decay_ref.shape[0]
    rate = decay_ref[...]

    def body(k, carry):
        state, total = carry
        base = pl.multiple_of(k * ROWS_PER_LOAD, ROWS_PER_LOAD)
        s_blk = _step_rows(raw_ref, bias_ref, base)
        x_blk = x_ref[pl.ds(base, ROWS_PER_LOAD), :].astype(jnp.float32)
        for i in range(ROWS_PER_LOAD):
            s_now = s_blk[i : i + 1]
            b_now = _lane_tile(b_ref[base + i], width)
            state = jnp.exp(-s_now * rate) * state + (s_now * x_blk[i : i + 1]) * b_now
        return state, total + jnp.sum(s_blk, axis=0, keepdims=True)

    zero = (jnp.zeros(rate.shape, jnp.float32), jnp.zeros((1, width), jnp.float32))
    state, total = lax.fori_loop(0, steps // ROWS_PER_LOAD, body, zero)
    state_ref[:states] = state
    state_ref[states:] = total


def _out_kernel(
    mine_ref, stacked_ref, raw_ref, bias_ref, x_ref, z_ref, decay_ref, b_ref, c_ref, skip_ref, gated_ref, y_ref
):
    steps, width = raw_ref.shape
    states = decay_ref.shape[0]
    rate = decay_ref[...]
    skip = skip_ref[...]
    mine = mine_ref[0]

    running = jnp.zeros(rate.shape, jnp.float32)
    for position in range(stacked_ref.shape[0] - 1):
        piece = stacked_ref[position]
        longer = jnp.exp(-rate * piece[states:]) * running + piece[:states]
        running = jnp.where(position < mine, longer, running)

    def body(k, state):
        base = pl.multiple_of(k * ROWS_PER_LOAD, ROWS_PER_LOAD)
        s_blk = _step_rows(raw_ref, bias_ref, base)
        x_blk = x_ref[pl.ds(base, ROWS_PER_LOAD), :].astype(jnp.float32)
        for i in range(ROWS_PER_LOAD):
            s_now = s_blk[i : i + 1]
            x_now = x_blk[i : i + 1]
            b_now = _lane_tile(b_ref[base + i], width)
            c_now = _lane_tile(c_ref[base + i], width)
            state = jnp.exp(-s_now * rate) * state + (s_now * x_now) * b_now
            y_ref[pl.ds(base + i, 1), :] = jnp.sum(c_now * state, axis=0, keepdims=True) + skip * x_now
        return state

    lax.fori_loop(0, steps // ROWS_PER_LOAD, body, running)
    z = z_ref[...].astype(jnp.float32)
    gated_ref[...] = (y_ref[...] * (z * jax.nn.sigmoid(z))).astype(gated_ref.dtype)


def _columns(b_coef, c_coef):
    rows = jnp.transpose(jnp.stack([b_coef, c_coef]).astype(jnp.float32), (0, 2, 1))
    return jnp.broadcast_to(rows[..., None], rows.shape + (LANES,))


def _coef_spec(steps, states, which):
    return pl.BlockSpec((None, steps, states, LANES), lambda j: (which, 0, 0, 0))


def scan_end(step_raw, step_bias, x_in, decay_rate, columns, width=1024):
    steps, chans = step_raw.shape
    states = decay_rate.shape[0]
    return pl.pallas_call(
        _end_kernel,
        grid=(chans // width,),
        in_specs=[
            pl.BlockSpec((steps, width), lambda j: (0, j)),
            pl.BlockSpec((1, width), lambda j: (0, j)),
            pl.BlockSpec((steps, width), lambda j: (0, j)),
            pl.BlockSpec((states, width), lambda j: (0, j)),
            _coef_spec(steps, states, 0),
        ],
        out_specs=pl.BlockSpec((states + 1, width), lambda j: (0, j)),
        out_shape=jax.ShapeDtypeStruct((states + 1, chans), jnp.float32),
        cost_estimate=pl.CostEstimate(
            flops=6 * steps * states * chans, transcendentals=steps * states * chans,
            bytes_accessed=steps * chans * 6 + states * chans * 8),
    )(step_raw, step_bias[None, :], x_in, decay_rate, columns)


def scan_gated(mine, stacked, step_raw, step_bias, x_in, z_in, decay_rate, columns, skip_gain, width=1024):
    steps, chans = step_raw.shape
    states = decay_rate.shape[0]
    count = stacked.shape[0]
    col = lambda j: (0, j)
    return pl.pallas_call(
        _out_kernel,
        grid=(chans // width,),
        in_specs=[
            pl.BlockSpec(memory_space=pltpu.SMEM),
            pl.BlockSpec((count, states + 1, width), lambda j: (0, 0, j)),
            pl.BlockSpec((steps, width), col),
            pl.BlockSpec((1, width), col),
            pl.BlockSpec((steps, width), col),
            pl.BlockSpec((steps, width), col),
            pl.BlockSpec((states, width), col),
            _coef_spec(steps, states, 0),
            _coef_spec(steps, states, 1),
            pl.BlockSpec((1, width), col),
        ],
        out_specs=pl.BlockSpec((steps, width), col),
        out_shape=jax.ShapeDtypeStruct((steps, chans), jnp.bfloat16),
        scratch_shapes=[pltpu.VMEM((steps, width), jnp.float32)],
        cost_estimate=pl.CostEstimate(
            flops=9 * steps * states * chans, transcendentals=steps * states * chans + steps * chans,
            bytes_accessed=steps * chans * 10 + count * states * chans * 4),
    )(mine, stacked, step_raw, step_bias[None, :], x_in, z_in, decay_rate, columns, columns, skip_gain[None, :])


def on_device(
    x_in,
    z_in,
    step_raw,
    step_bias,
    decay_rate,
    b_coef,
    c_coef,
    skip_gain,
    out_proj,
    residual,
    norm_gain,
    router_weight,
    expert_ids,
    gate_weight,
    up_weight,
    down_weight,
):
    columns = _columns(b_coef, c_coef)
    state_end = scan_end(step_raw, step_bias, x_in, decay_rate, columns)
    stacked = lax.all_gather(state_end, "seq")
    mine = lax.axis_index("seq").astype(jnp.int32).reshape(1)
    gated = scan_gated(mine, stacked, step_raw, step_bias, x_in, z_in, decay_rate, columns, skip_gain)
    seq_count = lax.axis_size("seq")
    expert_count = lax.axis_size("expert")
    rows = residual.shape[0]
    gathered = lax.all_gather(gated, "seq", axis=0, tiled=True)
    column_part = jnp.dot(gathered, out_proj, preferred_element_type=jnp.float32).astype(jnp.bfloat16)
    column_part = column_part.reshape(seq_count * expert_count, rows, column_part.shape[1])
    swapped = lax.all_to_all(column_part, ("seq", "expert"), split_axis=0, concat_axis=0, tiled=True)
    swapped = swapped.reshape(seq_count, expert_count, rows, column_part.shape[2])
    summed = jnp.sum(swapped.astype(jnp.float32), axis=1)
    mamba_out = jnp.transpose(summed, (1, 0, 2)).reshape(rows, -1)
    hidden = (residual.astype(jnp.float32) + mamba_out).astype(jnp.bfloat16)
    hidden_f = hidden.astype(jnp.float32)
    width_d = hidden.shape[1]
    scale_cols = width_d // BLOCK
    normed = (
        hidden_f
        * lax.rsqrt(jnp.mean(hidden_f * hidden_f, axis=-1, keepdims=True) + 1e-05)
        * norm_gain[None, :]
    )
    blocked = normed.reshape(rows, scale_cols, BLOCK)
    scales = (jnp.max(jnp.abs(blocked), axis=-1) / 448.0 + 1e-06).astype(jnp.bfloat16)
    quant = (blocked / scales.astype(jnp.float32)[..., None]).astype(jnp.bfloat16)
    restored = (
        (quant.astype(jnp.float32) * scales.astype(jnp.float32)[..., None])
        .astype(jnp.bfloat16)
        .reshape(rows, width_d)
    )
    experts = router_weight.shape[1]
    probs = jax.nn.sigmoid(jnp.dot(restored, router_weight, preferred_element_type=jnp.float32))
    picks = expert_ids[:, :, None] == jnp.arange(experts, dtype=jnp.int32)[None, None, :]
    chosen = jnp.sum(jnp.where(picks, probs[:, None, :], jnp.float32(0.0)), axis=-1)
    weights = chosen / jnp.sum(chosen, axis=-1, keepdims=True)
    coef = jnp.sum(jnp.where(expert_ids == 0, weights, jnp.float32(0.0)), axis=1)
    wanted = jnp.any(expert_ids == 0, axis=1)
    wanted_int = wanted.astype(jnp.int32)
    slot_pos = jnp.cumsum(wanted_int) - wanted_int
    capacity = rows // 2
    table = (
        (slot_pos[None, :] == jnp.arange(capacity, dtype=jnp.int32)[:, None]) & wanted[None, :]
    ).astype(jnp.bfloat16)
    send_rows = jnp.dot(table, restored, preferred_element_type=jnp.float32).astype(jnp.bfloat16)
    inputs = lax.all_gather(send_rows, ("seq", "expert"), axis=0, tiled=True)
    own_sum = lax.psum_scatter(
        expert_partial(inputs, gate_weight, up_weight, down_weight),
        ("seq", "expert"),
        scatter_dimension=0,
        tiled=True,
    )
    returned = jnp.dot(table.T, own_sum, preferred_element_type=jnp.float32)
    return (hidden_f + coef[:, None] * returned).astype(jnp.bfloat16)


def solution(mesh):
    return jax.shard_map(
        on_device,
        mesh=mesh,
        in_specs=(
            P(("dp", "seq"), "expert"),
            P(("dp", "seq"), "expert"),
            P(("dp", "seq"), "expert"),
            P("expert"),
            P(None, "expert"),
            P(None, ("dp", "seq")),
            P(None, ("dp", "seq")),
            P("expert"),
            P("expert", "seq"),
            P(("dp", "seq", "expert"), None),
            P(),
            P(),
            P(("dp", "seq", "expert"), None),
            P(None, ("seq", "expert")),
            P(None, ("seq", "expert")),
            P(("seq", "expert"), None),
        ),
        out_specs=P(("dp", "seq", "expert"), None),
        check_vma=False,
    )
```

```python
import jax
import jax.numpy as jnp
from jax import lax
from jax.experimental import pallas as pl
from jax.experimental.pallas import tpu as pltpu
from jax.sharding import PartitionSpec as P

BLOCK = 128
LANES = 128
ROWS_PER_LOAD = 16

EXPERT_TILE = 2048


def _expert_kernel(nk, rows_ref, gate_ref, up_ref, down_ref, out_ref, acc_g, acc_u, active):
    i = pl.program_id(0)

    @pl.when(i == 0)
    def _():
        acc_g[...] = jnp.zeros_like(acc_g)
        acc_u[...] = jnp.zeros_like(acc_u)

    @pl.when(i < nk)
    def _():
        x = rows_ref[...]
        acc_g[...] += jnp.dot(x, gate_ref[...], preferred_element_type=jnp.float32)
        acc_u[...] += jnp.dot(x, up_ref[...], preferred_element_type=jnp.float32)

    @pl.when(i == nk - 1)
    def _():
        g = acc_g[...]
        active[...] = (g * jax.nn.sigmoid(g) * acc_u[...]).astype(active.dtype)

    @pl.when(i >= nk)
    def _():
        out_ref[...] = jnp.dot(active[...], down_ref[...], preferred_element_type=jnp.float32).astype(
            out_ref.dtype
        )


def expert_partial(inputs, gate_weight, up_weight, down_weight):
    slots, width = inputs.shape
    hidden = gate_weight.shape[1]
    tile, k_tile = EXPERT_TILE, EXPERT_TILE // 2
    nk, nn = width // k_tile, down_weight.shape[1] // tile
    k_of = lambda i: jnp.minimum(i, nk - 1)
    n_of = lambda i: jnp.maximum(i - nk, 0)
    return pl.pallas_call(
        lambda *refs: _expert_kernel(nk, *refs),
        grid=(nk + nn,),
        in_specs=[
            pl.BlockSpec((slots, k_tile), lambda i: (0, k_of(i))),
            pl.BlockSpec((k_tile, hidden), lambda i: (k_of(i), 0)),
            pl.BlockSpec((k_tile, hidden), lambda i: (k_of(i), 0)),
            pl.BlockSpec((hidden, tile), lambda i: (0, n_of(i))),
        ],
        out_specs=pl.BlockSpec((slots, tile), lambda i: (0, n_of(i))),
        out_shape=jax.ShapeDtypeStruct((slots, down_weight.shape[1]), jnp.bfloat16),
        scratch_shapes=[
            pltpu.VMEM((slots, hidden), jnp.float32),
            pltpu.VMEM((slots, hidden), jnp.float32),
            pltpu.VMEM((slots, hidden), jnp.bfloat16),
        ],
        compiler_params=pltpu.CompilerParams(
            dimension_semantics=("arbitrary",), vmem_limit_bytes=48 * 1024 * 1024
        ),
        cost_estimate=pl.CostEstimate(
            flops=6 * slots * width * hidden,
            transcendentals=slots * hidden,
            bytes_accessed=2 * (2 * slots * width + 3 * width * hidden),
        ),
    )(inputs, gate_weight, up_weight, down_weight)


def _lane_tile(col, width):
    return jnp.concatenate([col] * (width // LANES), axis=1) if width > LANES else col


def _step_rows(raw_ref, bias_ref, base):
    raw = raw_ref[pl.ds(base, ROWS_PER_LOAD), :].astype(jnp.float32)
    return jax.nn.softplus(raw + bias_ref[...])


def _end_kernel(raw_ref, bias_ref, x_ref, decay_ref, b_ref, state_ref):
    steps, width = raw_ref.shape
    states = decay_ref.shape[0]
    rate = decay_ref[...]

    def body(k, carry):
        state, total = carry
        base = pl.multiple_of(k * ROWS_PER_LOAD, ROWS_PER_LOAD)
        s_blk = _step_rows(raw_ref, bias_ref, base)
        x_blk = x_ref[pl.ds(base, ROWS_PER_LOAD), :].astype(jnp.float32)
        for i in range(ROWS_PER_LOAD):
            s_now = s_blk[i : i + 1]
            b_now = _lane_tile(b_ref[base + i], width)
            state = jnp.exp(-s_now * rate) * state + (s_now * x_blk[i : i + 1]) * b_now
        return state, total + jnp.sum(s_blk, axis=0, keepdims=True)

    zero = (jnp.zeros(rate.shape, jnp.float32), jnp.zeros((1, width), jnp.float32))
    state, total = lax.fori_loop(0, steps // ROWS_PER_LOAD, body, zero)
    state_ref[:states] = state
    state_ref[states:] = total


def _out_kernel(
    mine_ref, stacked_ref, raw_ref, bias_ref, x_ref, z_ref, decay_ref, b_ref, c_ref, skip_ref, gated_ref, y_ref
):
    steps, width = raw_ref.shape
    states = decay_ref.shape[0]
    rate = decay_ref[...]
    skip = skip_ref[...]
    mine = mine_ref[0]

    running = jnp.zeros(rate.shape, jnp.float32)
    for position in range(stacked_ref.shape[0] - 1):
        piece = stacked_ref[position]
        longer = jnp.exp(-rate * piece[states:]) * running + piece[:states]
        running = jnp.where(position < mine, longer, running)

    def body(k, state):
        base = pl.multiple_of(k * ROWS_PER_LOAD, ROWS_PER_LOAD)
        s_blk = _step_rows(raw_ref, bias_ref, base)
        x_blk = x_ref[pl.ds(base, ROWS_PER_LOAD), :].astype(jnp.float32)
        for i in range(ROWS_PER_LOAD):
            s_now = s_blk[i : i + 1]
            x_now = x_blk[i : i + 1]
            b_now = _lane_tile(b_ref[base + i], width)
            c_now = _lane_tile(c_ref[base + i], width)
            state = jnp.exp(-s_now * rate) * state + (s_now * x_now) * b_now
            y_ref[pl.ds(base + i, 1), :] = jnp.sum(c_now * state, axis=0, keepdims=True) + skip * x_now
        return state

    lax.fori_loop(0, steps // ROWS_PER_LOAD, body, running)
    z = z_ref[...].astype(jnp.float32)
    gated_ref[...] = (y_ref[...] * (z * jax.nn.sigmoid(z))).astype(gated_ref.dtype)


def _columns(b_coef, c_coef):
    rows = jnp.transpose(jnp.stack([b_coef, c_coef]).astype(jnp.float32), (0, 2, 1))
    return jnp.broadcast_to(rows[..., None], rows.shape + (LANES,))


def _coef_spec(steps, states, which):
    return pl.BlockSpec((None, steps, states, LANES), lambda j: (which, 0, 0, 0))


def scan_end(step_raw, step_bias, x_in, decay_rate, columns, width=512):
    steps, chans = step_raw.shape
    states = decay_rate.shape[0]
    return pl.pallas_call(
        _end_kernel,
        grid=(chans // width,),
        in_specs=[
            pl.BlockSpec((steps, width), lambda j: (0, j)),
            pl.BlockSpec((1, width), lambda j: (0, j)),
            pl.BlockSpec((steps, width), lambda j: (0, j)),
            pl.BlockSpec((states, width), lambda j: (0, j)),
            _coef_spec(steps, states, 0),
        ],
        out_specs=pl.BlockSpec((states + 1, width), lambda j: (0, j)),
        out_shape=jax.ShapeDtypeStruct((states + 1, chans), jnp.float32),
        cost_estimate=pl.CostEstimate(
            flops=6 * steps * states * chans, transcendentals=steps * states * chans,
            bytes_accessed=steps * chans * 6 + states * chans * 8),
    )(step_raw, step_bias[None, :], x_in, decay_rate, columns)


def scan_gated(mine, stacked, step_raw, step_bias, x_in, z_in, decay_rate, columns, skip_gain, width=512):
    steps, chans = step_raw.shape
    states = decay_rate.shape[0]
    count = stacked.shape[0]
    col = lambda j: (0, j)
    return pl.pallas_call(
        _out_kernel,
        grid=(chans // width,),
        in_specs=[
            pl.BlockSpec(memory_space=pltpu.SMEM),
            pl.BlockSpec((count, states + 1, width), lambda j: (0, 0, j)),
            pl.BlockSpec((steps, width), col),
            pl.BlockSpec((1, width), col),
            pl.BlockSpec((steps, width), col),
            pl.BlockSpec((steps, width), col),
            pl.BlockSpec((states, width), col),
            _coef_spec(steps, states, 0),
            _coef_spec(steps, states, 1),
            pl.BlockSpec((1, width), col),
        ],
        out_specs=pl.BlockSpec((steps, width), col),
        out_shape=jax.ShapeDtypeStruct((steps, chans), jnp.bfloat16),
        scratch_shapes=[pltpu.VMEM((steps, width), jnp.float32)],
        cost_estimate=pl.CostEstimate(
            flops=9 * steps * states * chans, transcendentals=steps * states * chans + steps * chans,
            bytes_accessed=steps * chans * 10 + count * states * chans * 4),
    )(mine, stacked, step_raw, step_bias[None, :], x_in, z_in, decay_rate, columns, columns, skip_gain[None, :])


def on_device(
    x_in,
    z_in,
    step_raw,
    step_bias,
    decay_rate,
    b_coef,
    c_coef,
    skip_gain,
    out_proj,
    residual,
    norm_gain,
    router_weight,
    expert_ids,
    gate_weight,
    up_weight,
    down_weight,
):
    columns = _columns(b_coef, c_coef)
    state_end = scan_end(step_raw, step_bias, x_in, decay_rate, columns)
    stacked = lax.all_gather(state_end, "seq")
    mine = lax.axis_index("seq").astype(jnp.int32).reshape(1)
    gated = scan_gated(mine, stacked, step_raw, step_bias, x_in, z_in, decay_rate, columns, skip_gain)
    seq_count = lax.axis_size("seq")
    expert_count = lax.axis_size("expert")
    rows = residual.shape[0]
    gathered = lax.all_gather(gated, "seq", axis=0, tiled=True)
    column_part = jnp.dot(gathered, out_proj, preferred_element_type=jnp.float32).astype(jnp.bfloat16)
    column_part = column_part.reshape(seq_count * expert_count, rows, column_part.shape[1])
    swapped = lax.all_to_all(column_part, ("seq", "expert"), split_axis=0, concat_axis=0, tiled=True)
    swapped = swapped.reshape(seq_count, expert_count, rows, column_part.shape[2])
    summed = jnp.sum(swapped.astype(jnp.float32), axis=1)
    mamba_out = jnp.transpose(summed, (1, 0, 2)).reshape(rows, -1)
    hidden = (residual.astype(jnp.float32) + mamba_out).astype(jnp.bfloat16)
    hidden_f = hidden.astype(jnp.float32)
    width_d = hidden.shape[1]
    scale_cols = width_d // BLOCK
    normed = (
        hidden_f
        * lax.rsqrt(jnp.mean(hidden_f * hidden_f, axis=-1, keepdims=True) + 1e-05)
        * norm_gain[None, :]
    )
    blocked = normed.reshape(rows, scale_cols, BLOCK)
    scales = (jnp.max(jnp.abs(blocked), axis=-1) / 448.0 + 1e-06).astype(jnp.bfloat16)
    quant = (blocked / scales.astype(jnp.float32)[..., None]).astype(jnp.bfloat16)
    restored = (
        (quant.astype(jnp.float32) * scales.astype(jnp.float32)[..., None])
        .astype(jnp.bfloat16)
        .reshape(rows, width_d)
    )
    experts = router_weight.shape[1]
    probs = jax.nn.sigmoid(jnp.dot(restored, router_weight, preferred_element_type=jnp.float32))
    picks = expert_ids[:, :, None] == jnp.arange(experts, dtype=jnp.int32)[None, None, :]
    chosen = jnp.sum(jnp.where(picks, probs[:, None, :], jnp.float32(0.0)), axis=-1)
    weights = chosen / jnp.sum(chosen, axis=-1, keepdims=True)
    coef = jnp.sum(jnp.where(expert_ids == 0, weights, jnp.float32(0.0)), axis=1)
    wanted = jnp.any(expert_ids == 0, axis=1)
    wanted_int = wanted.astype(jnp.int32)
    slot_pos = jnp.cumsum(wanted_int) - wanted_int
    capacity = rows // 2
    table = (
        (slot_pos[None, :] == jnp.arange(capacity, dtype=jnp.int32)[:, None]) & wanted[None, :]
    ).astype(jnp.bfloat16)
    send_rows = jnp.dot(table, restored, preferred_element_type=jnp.float32).astype(jnp.bfloat16)
    inputs = lax.all_gather(send_rows, ("seq", "expert"), axis=0, tiled=True)
    own_sum = lax.psum_scatter(
        expert_partial(inputs, gate_weight, up_weight, down_weight),
        ("seq", "expert"),
        scatter_dimension=0,
        tiled=True,
    )
    returned = jnp.dot(table.T, own_sum, preferred_element_type=jnp.float32)
    return (hidden_f + coef[:, None] * returned).astype(jnp.bfloat16)


def solution(mesh):
    return jax.shard_map(
        on_device,
        mesh=mesh,
        in_specs=(
            P(("dp", "seq"), "expert"),
            P(("dp", "seq"), "expert"),
            P(("dp", "seq"), "expert"),
            P("expert"),
            P(None, "expert"),
            P(None, ("dp", "seq")),
            P(None, ("dp", "seq")),
            P("expert"),
            P("expert", "seq"),
            P(("dp", "seq", "expert"), None),
            P(),
            P(),
            P(("dp", "seq", "expert"), None),
            P(None, ("seq", "expert")),
            P(None, ("seq", "expert")),
            P(("seq", "expert"), None),
        ),
        out_specs=P(("dp", "seq", "expert"), None),
        check_vma=False,
    )
```

```python
import jax
import jax.numpy as jnp
from jax import lax
from jax.experimental import pallas as pl
from jax.experimental.pallas import tpu as pltpu
from jax.sharding import PartitionSpec as P

BLOCK = 128
LANES = 128
ROWS_PER_LOAD = 16

EXPERT_TILE = 2048


def _expert_kernel(nk, rows_ref, gate_ref, up_ref, down_ref, out_ref, acc_g, acc_u, active):
    i = pl.program_id(0)

    @pl.when(i == 0)
    def _():
        acc_g[...] = jnp.zeros_like(acc_g)
        acc_u[...] = jnp.zeros_like(acc_u)

    @pl.when(i < nk)
    def _():
        x = rows_ref[...]
        acc_g[...] += jnp.dot(x, gate_ref[...], preferred_element_type=jnp.float32)
        acc_u[...] += jnp.dot(x, up_ref[...], preferred_element_type=jnp.float32)

    @pl.when(i == nk - 1)
    def _():
        g = acc_g[...]
        active[...] = (g * jax.nn.sigmoid(g) * acc_u[...]).astype(active.dtype)

    @pl.when(i >= nk)
    def _():
        out_ref[...] = jnp.dot(active[...], down_ref[...], preferred_element_type=jnp.float32).astype(
            out_ref.dtype
        )


def expert_partial(inputs, gate_weight, up_weight, down_weight):
    slots, width = inputs.shape
    hidden = gate_weight.shape[1]
    tile, k_tile = EXPERT_TILE, EXPERT_TILE * 2
    nk, nn = width // k_tile, down_weight.shape[1] // tile
    k_of = lambda i: jnp.minimum(i, nk - 1)
    n_of = lambda i: jnp.maximum(i - nk, 0)
    return pl.pallas_call(
        lambda *refs: _expert_kernel(nk, *refs),
        grid=(nk + nn,),
        in_specs=[
            pl.BlockSpec((slots, k_tile), lambda i: (0, k_of(i))),
            pl.BlockSpec((k_tile, hidden), lambda i: (k_of(i), 0)),
            pl.BlockSpec((k_tile, hidden), lambda i: (k_of(i), 0)),
            pl.BlockSpec((hidden, tile), lambda i: (0, n_of(i))),
        ],
        out_specs=pl.BlockSpec((slots, tile), lambda i: (0, n_of(i))),
        out_shape=jax.ShapeDtypeStruct((slots, down_weight.shape[1]), jnp.bfloat16),
        scratch_shapes=[
            pltpu.VMEM((slots, hidden), jnp.float32),
            pltpu.VMEM((slots, hidden), jnp.float32),
            pltpu.VMEM((slots, hidden), jnp.bfloat16),
        ],
        compiler_params=pltpu.CompilerParams(
            dimension_semantics=("arbitrary",), vmem_limit_bytes=48 * 1024 * 1024
        ),
        cost_estimate=pl.CostEstimate(
            flops=6 * slots * width * hidden,
            transcendentals=slots * hidden,
            bytes_accessed=2 * (2 * slots * width + 3 * width * hidden),
        ),
    )(inputs, gate_weight, up_weight, down_weight)


def _lane_tile(col, width):
    return jnp.concatenate([col] * (width // LANES), axis=1) if width > LANES else col


def _step_rows(raw_ref, bias_ref, base):
    raw = raw_ref[pl.ds(base, ROWS_PER_LOAD), :].astype(jnp.float32)
    return jax.nn.softplus(raw + bias_ref[...])


def _end_kernel(raw_ref, bias_ref, x_ref, decay_ref, b_ref, state_ref):
    steps, width = raw_ref.shape
    states = decay_ref.shape[0]
    rate = decay_ref[...]

    def body(k, carry):
        state, total = carry
        base = pl.multiple_of(k * ROWS_PER_LOAD, ROWS_PER_LOAD)
        s_blk = _step_rows(raw_ref, bias_ref, base)
        x_blk = x_ref[pl.ds(base, ROWS_PER_LOAD), :].astype(jnp.float32)
        for i in range(ROWS_PER_LOAD):
            s_now = s_blk[i : i + 1]
            b_now = _lane_tile(b_ref[base + i], width)
            state = jnp.exp(-s_now * rate) * state + (s_now * x_blk[i : i + 1]) * b_now
        return state, total + jnp.sum(s_blk, axis=0, keepdims=True)

    zero = (jnp.zeros(rate.shape, jnp.float32), jnp.zeros((1, width), jnp.float32))
    state, total = lax.fori_loop(0, steps // ROWS_PER_LOAD, body, zero)
    state_ref[:states] = state
    state_ref[states:] = total


def _out_kernel(
    mine_ref, stacked_ref, raw_ref, bias_ref, x_ref, z_ref, decay_ref, b_ref, c_ref, skip_ref, gated_ref, y_ref
):
    steps, width = raw_ref.shape
    states = decay_ref.shape[0]
    rate = decay_ref[...]
    skip = skip_ref[...]
    mine = mine_ref[0]

    running = jnp.zeros(rate.shape, jnp.float32)
    for position in range(stacked_ref.shape[0] - 1):
        piece = stacked_ref[position]
        longer = jnp.exp(-rate * piece[states:]) * running + piece[:states]
        running = jnp.where(position < mine, longer, running)

    def body(k, state):
        base = pl.multiple_of(k * ROWS_PER_LOAD, ROWS_PER_LOAD)
        s_blk = _step_rows(raw_ref, bias_ref, base)
        x_blk = x_ref[pl.ds(base, ROWS_PER_LOAD), :].astype(jnp.float32)
        for i in range(ROWS_PER_LOAD):
            s_now = s_blk[i : i + 1]
            x_now = x_blk[i : i + 1]
            b_now = _lane_tile(b_ref[base + i], width)
            c_now = _lane_tile(c_ref[base + i], width)
            state = jnp.exp(-s_now * rate) * state + (s_now * x_now) * b_now
            y_ref[pl.ds(base + i, 1), :] = jnp.sum(c_now * state, axis=0, keepdims=True) + skip * x_now
        return state

    lax.fori_loop(0, steps // ROWS_PER_LOAD, body, running)
    z = z_ref[...].astype(jnp.float32)
    gated_ref[...] = (y_ref[...] * (z * jax.nn.sigmoid(z))).astype(gated_ref.dtype)


def _columns(b_coef, c_coef):
    rows = jnp.transpose(jnp.stack([b_coef, c_coef]).astype(jnp.float32), (0, 2, 1))
    return jnp.broadcast_to(rows[..., None], rows.shape + (LANES,))


def _coef_spec(steps, states, which):
    return pl.BlockSpec((None, steps, states, LANES), lambda j: (which, 0, 0, 0))


def scan_end(step_raw, step_bias, x_in, decay_rate, columns, width=512):
    steps, chans = step_raw.shape
    states = decay_rate.shape[0]
    return pl.pallas_call(
        _end_kernel,
        grid=(chans // width,),
        in_specs=[
            pl.BlockSpec((steps, width), lambda j: (0, j)),
            pl.BlockSpec((1, width), lambda j: (0, j)),
            pl.BlockSpec((steps, width), lambda j: (0, j)),
            pl.BlockSpec((states, width), lambda j: (0, j)),
            _coef_spec(steps, states, 0),
        ],
        out_specs=pl.BlockSpec((states + 1, width), lambda j: (0, j)),
        out_shape=jax.ShapeDtypeStruct((states + 1, chans), jnp.float32),
        cost_estimate=pl.CostEstimate(
            flops=6 * steps * states * chans, transcendentals=steps * states * chans,
            bytes_accessed=steps * chans * 6 + states * chans * 8),
    )(step_raw, step_bias[None, :], x_in, decay_rate, columns)


def scan_gated(mine, stacked, step_raw, step_bias, x_in, z_in, decay_rate, columns, skip_gain, width=512):
    steps, chans = step_raw.shape
    states = decay_rate.shape[0]
    count = stacked.shape[0]
    col = lambda j: (0, j)
    return pl.pallas_call(
        _out_kernel,
        grid=(chans // width,),
        in_specs=[
            pl.BlockSpec(memory_space=pltpu.SMEM),
            pl.BlockSpec((count, states + 1, width), lambda j: (0, 0, j)),
            pl.BlockSpec((steps, width), col),
            pl.BlockSpec((1, width), col),
            pl.BlockSpec((steps, width), col),
            pl.BlockSpec((steps, width), col),
            pl.BlockSpec((states, width), col),
            _coef_spec(steps, states, 0),
            _coef_spec(steps, states, 1),
            pl.BlockSpec((1, width), col),
        ],
        out_specs=pl.BlockSpec((steps, width), col),
        out_shape=jax.ShapeDtypeStruct((steps, chans), jnp.bfloat16),
        scratch_shapes=[pltpu.VMEM((steps, width), jnp.float32)],
        cost_estimate=pl.CostEstimate(
            flops=9 * steps * states * chans, transcendentals=steps * states * chans + steps * chans,
            bytes_accessed=steps * chans * 10 + count * states * chans * 4),
    )(mine, stacked, step_raw, step_bias[None, :], x_in, z_in, decay_rate, columns, columns, skip_gain[None, :])


def on_device(
    x_in,
    z_in,
    step_raw,
    step_bias,
    decay_rate,
    b_coef,
    c_coef,
    skip_gain,
    out_proj,
    residual,
    norm_gain,
    router_weight,
    expert_ids,
    gate_weight,
    up_weight,
    down_weight,
):
    columns = _columns(b_coef, c_coef)
    state_end = scan_end(step_raw, step_bias, x_in, decay_rate, columns)
    stacked = lax.all_gather(state_end, "seq")
    mine = lax.axis_index("seq").astype(jnp.int32).reshape(1)
    gated = scan_gated(mine, stacked, step_raw, step_bias, x_in, z_in, decay_rate, columns, skip_gain)
    seq_count = lax.axis_size("seq")
    expert_count = lax.axis_size("expert")
    rows = residual.shape[0]
    gathered = lax.all_gather(gated, "seq", axis=0, tiled=True)
    column_part = jnp.dot(gathered, out_proj, preferred_element_type=jnp.float32).astype(jnp.bfloat16)
    column_part = column_part.reshape(seq_count * expert_count, rows, column_part.shape[1])
    swapped = lax.all_to_all(column_part, ("seq", "expert"), split_axis=0, concat_axis=0, tiled=True)
    swapped = swapped.reshape(seq_count, expert_count, rows, column_part.shape[2])
    summed = jnp.sum(swapped.astype(jnp.float32), axis=1)
    mamba_out = jnp.transpose(summed, (1, 0, 2)).reshape(rows, -1)
    hidden = (residual.astype(jnp.float32) + mamba_out).astype(jnp.bfloat16)
    hidden_f = hidden.astype(jnp.float32)
    width_d = hidden.shape[1]
    scale_cols = width_d // BLOCK
    normed = (
        hidden_f
        * lax.rsqrt(jnp.mean(hidden_f * hidden_f, axis=-1, keepdims=True) + 1e-05)
        * norm_gain[None, :]
    )
    blocked = normed.reshape(rows, scale_cols, BLOCK)
    scales = (jnp.max(jnp.abs(blocked), axis=-1) / 448.0 + 1e-06).astype(jnp.bfloat16)
    quant = (blocked / scales.astype(jnp.float32)[..., None]).astype(jnp.bfloat16)
    restored = (
        (quant.astype(jnp.float32) * scales.astype(jnp.float32)[..., None])
        .astype(jnp.bfloat16)
        .reshape(rows, width_d)
    )
    experts = router_weight.shape[1]
    probs = jax.nn.sigmoid(jnp.dot(restored, router_weight, preferred_element_type=jnp.float32))
    picks = expert_ids[:, :, None] == jnp.arange(experts, dtype=jnp.int32)[None, None, :]
    chosen = jnp.sum(jnp.where(picks, probs[:, None, :], jnp.float32(0.0)), axis=-1)
    weights = chosen / jnp.sum(chosen, axis=-1, keepdims=True)
    coef = jnp.sum(jnp.where(expert_ids == 0, weights, jnp.float32(0.0)), axis=1)
    wanted = jnp.any(expert_ids == 0, axis=1)
    wanted_int = wanted.astype(jnp.int32)
    slot_pos = jnp.cumsum(wanted_int) - wanted_int
    capacity = rows // 2
    table = (
        (slot_pos[None, :] == jnp.arange(capacity, dtype=jnp.int32)[:, None]) & wanted[None, :]
    ).astype(jnp.bfloat16)
    send_rows = jnp.dot(table, restored, preferred_element_type=jnp.float32).astype(jnp.bfloat16)
    inputs = lax.all_gather(send_rows, ("seq", "expert"), axis=0, tiled=True)
    own_sum = lax.psum_scatter(
        expert_partial(inputs, gate_weight, up_weight, down_weight),
        ("seq", "expert"),
        scatter_dimension=0,
        tiled=True,
    )
    returned = jnp.dot(table.T, own_sum, preferred_element_type=jnp.float32)
    return (hidden_f + coef[:, None] * returned).astype(jnp.bfloat16)


def solution(mesh):
    return jax.shard_map(
        on_device,
        mesh=mesh,
        in_specs=(
            P(("dp", "seq"), "expert"),
            P(("dp", "seq"), "expert"),
            P(("dp", "seq"), "expert"),
            P("expert"),
            P(None, "expert"),
            P(None, ("dp", "seq")),
            P(None, ("dp", "seq")),
            P("expert"),
            P("expert", "seq"),
            P(("dp", "seq", "expert"), None),
            P(),
            P(),
            P(("dp", "seq", "expert"), None),
            P(None, ("seq", "expert")),
            P(None, ("seq", "expert")),
            P(("seq", "expert"), None),
        ),
        out_specs=P(("dp", "seq", "expert"), None),
        check_vma=False,
    )
```

```python
import jax
import jax.numpy as jnp
from jax import lax
from jax.experimental import pallas as pl
from jax.experimental.pallas import tpu as pltpu
from jax.sharding import PartitionSpec as P

BLOCK = 128
LANES = 128
ROWS_PER_LOAD = 32

EXPERT_TILE = 2048


def _expert_kernel(nk, rows_ref, gate_ref, up_ref, down_ref, out_ref, acc_g, acc_u, active):
    i = pl.program_id(0)

    @pl.when(i == 0)
    def _():
        acc_g[...] = jnp.zeros_like(acc_g)
        acc_u[...] = jnp.zeros_like(acc_u)

    @pl.when(i < nk)
    def _():
        x = rows_ref[...]
        acc_g[...] += jnp.dot(x, gate_ref[...], preferred_element_type=jnp.float32)
        acc_u[...] += jnp.dot(x, up_ref[...], preferred_element_type=jnp.float32)

    @pl.when(i == nk - 1)
    def _():
        g = acc_g[...]
        active[...] = (g * jax.nn.sigmoid(g) * acc_u[...]).astype(active.dtype)

    @pl.when(i >= nk)
    def _():
        out_ref[...] = jnp.dot(active[...], down_ref[...], preferred_element_type=jnp.float32).astype(
            out_ref.dtype
        )


def expert_partial(inputs, gate_weight, up_weight, down_weight):
    slots, width = inputs.shape
    hidden = gate_weight.shape[1]
    tile = EXPERT_TILE
    nk, nn = width // tile, down_weight.shape[1] // tile
    k_of = lambda i: jnp.minimum(i, nk - 1)
    n_of = lambda i: jnp.maximum(i - nk, 0)
    return pl.pallas_call(
        lambda *refs: _expert_kernel(nk, *refs),
        grid=(nk + nn,),
        in_specs=[
            pl.BlockSpec((slots, tile), lambda i: (0, k_of(i))),
            pl.BlockSpec((tile, hidden), lambda i: (k_of(i), 0)),
            pl.BlockSpec((tile, hidden), lambda i: (k_of(i), 0)),
            pl.BlockSpec((hidden, tile), lambda i: (0, n_of(i))),
        ],
        out_specs=pl.BlockSpec((slots, tile), lambda i: (0, n_of(i))),
        out_shape=jax.ShapeDtypeStruct((slots, down_weight.shape[1]), jnp.bfloat16),
        scratch_shapes=[
            pltpu.VMEM((slots, hidden), jnp.float32),
            pltpu.VMEM((slots, hidden), jnp.float32),
            pltpu.VMEM((slots, hidden), jnp.bfloat16),
        ],
        compiler_params=pltpu.CompilerParams(
            dimension_semantics=("arbitrary",), vmem_limit_bytes=48 * 1024 * 1024
        ),
        cost_estimate=pl.CostEstimate(
            flops=6 * slots * width * hidden,
            transcendentals=slots * hidden,
            bytes_accessed=2 * (2 * slots * width + 3 * width * hidden),
        ),
    )(inputs, gate_weight, up_weight, down_weight)


def _lane_tile(col, width):
    return jnp.concatenate([col] * (width // LANES), axis=1) if width > LANES else col


def _step_rows(raw_ref, bias_ref, base):
    raw = raw_ref[pl.ds(base, ROWS_PER_LOAD), :].astype(jnp.float32)
    return jax.nn.softplus(raw + bias_ref[...])


def _end_kernel(raw_ref, bias_ref, x_ref, decay_ref, b_ref, state_ref):
    steps, width = raw_ref.shape
    states = decay_ref.shape[0]
    rate = decay_ref[...]

    def body(k, carry):
        state, total = carry
        base = pl.multiple_of(k * ROWS_PER_LOAD, ROWS_PER_LOAD)
        s_blk = _step_rows(raw_ref, bias_ref, base)
        x_blk = x_ref[pl.ds(base, ROWS_PER_LOAD), :].astype(jnp.float32)
        for i in range(ROWS_PER_LOAD):
            s_now = s_blk[i : i + 1]
            b_now = _lane_tile(b_ref[base + i], width)
            state = jnp.exp(-s_now * rate) * state + (s_now * x_blk[i : i + 1]) * b_now
        return state, total + jnp.sum(s_blk, axis=0, keepdims=True)

    zero = (jnp.zeros(rate.shape, jnp.float32), jnp.zeros((1, width), jnp.float32))
    state, total = lax.fori_loop(0, steps // ROWS_PER_LOAD, body, zero)
    state_ref[:states] = state
    state_ref[states:] = total


def _out_kernel(
    mine_ref, stacked_ref, raw_ref, bias_ref, x_ref, z_ref, decay_ref, b_ref, c_ref, skip_ref, gated_ref, y_ref
):
    steps, width = raw_ref.shape
    states = decay_ref.shape[0]
    rate = decay_ref[...]
    skip = skip_ref[...]
    mine = mine_ref[0]

    running = jnp.zeros(rate.shape, jnp.float32)
    for position in range(stacked_ref.shape[0] - 1):
        piece = stacked_ref[position]
        longer = jnp.exp(-rate * piece[states:]) * running + piece[:states]
        running = jnp.where(position < mine, longer, running)

    def body(k, state):
        base = pl.multiple_of(k * ROWS_PER_LOAD, ROWS_PER_LOAD)
        s_blk = _step_rows(raw_ref, bias_ref, base)
        x_blk = x_ref[pl.ds(base, ROWS_PER_LOAD), :].astype(jnp.float32)
        for i in range(ROWS_PER_LOAD):
            s_now = s_blk[i : i + 1]
            x_now = x_blk[i : i + 1]
            b_now = _lane_tile(b_ref[base + i], width)
            c_now = _lane_tile(c_ref[base + i], width)
            state = jnp.exp(-s_now * rate) * state + (s_now * x_now) * b_now
            y_ref[pl.ds(base + i, 1), :] = jnp.sum(c_now * state, axis=0, keepdims=True) + skip * x_now
        return state

    lax.fori_loop(0, steps // ROWS_PER_LOAD, body, running)
    z = z_ref[...].astype(jnp.float32)
    gated_ref[...] = (y_ref[...] * (z * jax.nn.sigmoid(z))).astype(gated_ref.dtype)


def _columns(b_coef, c_coef):
    rows = jnp.transpose(jnp.stack([b_coef, c_coef]).astype(jnp.float32), (0, 2, 1))
    return jnp.broadcast_to(rows[..., None], rows.shape + (LANES,))


def _coef_spec(steps, states, which):
    return pl.BlockSpec((None, steps, states, LANES), lambda j: (which, 0, 0, 0))


def scan_end(step_raw, step_bias, x_in, decay_rate, columns, width=512):
    steps, chans = step_raw.shape
    states = decay_rate.shape[0]
    return pl.pallas_call(
        _end_kernel,
        grid=(chans // width,),
        in_specs=[
            pl.BlockSpec((steps, width), lambda j: (0, j)),
            pl.BlockSpec((1, width), lambda j: (0, j)),
            pl.BlockSpec((steps, width), lambda j: (0, j)),
            pl.BlockSpec((states, width), lambda j: (0, j)),
            _coef_spec(steps, states, 0),
        ],
        out_specs=pl.BlockSpec((states + 1, width), lambda j: (0, j)),
        out_shape=jax.ShapeDtypeStruct((states + 1, chans), jnp.float32),
        cost_estimate=pl.CostEstimate(
            flops=6 * steps * states * chans, transcendentals=steps * states * chans,
            bytes_accessed=steps * chans * 6 + states * chans * 8),
    )(step_raw, step_bias[None, :], x_in, decay_rate, columns)


def scan_gated(mine, stacked, step_raw, step_bias, x_in, z_in, decay_rate, columns, skip_gain, width=512):
    steps, chans = step_raw.shape
    states = decay_rate.shape[0]
    count = stacked.shape[0]
    col = lambda j: (0, j)
    return pl.pallas_call(
        _out_kernel,
        grid=(chans // width,),
        in_specs=[
            pl.BlockSpec(memory_space=pltpu.SMEM),
            pl.BlockSpec((count, states + 1, width), lambda j: (0, 0, j)),
            pl.BlockSpec((steps, width), col),
            pl.BlockSpec((1, width), col),
            pl.BlockSpec((steps, width), col),
            pl.BlockSpec((steps, width), col),
            pl.BlockSpec((states, width), col),
            _coef_spec(steps, states, 0),
            _coef_spec(steps, states, 1),
            pl.BlockSpec((1, width), col),
        ],
        out_specs=pl.BlockSpec((steps, width), col),
        out_shape=jax.ShapeDtypeStruct((steps, chans), jnp.bfloat16),
        scratch_shapes=[pltpu.VMEM((steps, width), jnp.float32)],
        cost_estimate=pl.CostEstimate(
            flops=9 * steps * states * chans, transcendentals=steps * states * chans + steps * chans,
            bytes_accessed=steps * chans * 10 + count * states * chans * 4),
    )(mine, stacked, step_raw, step_bias[None, :], x_in, z_in, decay_rate, columns, columns, skip_gain[None, :])


def on_device(
    x_in,
    z_in,
    step_raw,
    step_bias,
    decay_rate,
    b_coef,
    c_coef,
    skip_gain,
    out_proj,
    residual,
    norm_gain,
    router_weight,
    expert_ids,
    gate_weight,
    up_weight,
    down_weight,
):
    columns = _columns(b_coef, c_coef)
    state_end = scan_end(step_raw, step_bias, x_in, decay_rate, columns)
    stacked = lax.all_gather(state_end, "seq")
    mine = lax.axis_index("seq").astype(jnp.int32).reshape(1)
    gated = scan_gated(mine, stacked, step_raw, step_bias, x_in, z_in, decay_rate, columns, skip_gain)
    seq_count = lax.axis_size("seq")
    expert_count = lax.axis_size("expert")
    rows = residual.shape[0]
    gathered = lax.all_gather(gated, "seq", axis=0, tiled=True)
    column_part = jnp.dot(gathered, out_proj, preferred_element_type=jnp.float32).astype(jnp.bfloat16)
    column_part = column_part.reshape(seq_count * expert_count, rows, column_part.shape[1])
    swapped = lax.all_to_all(column_part, ("seq", "expert"), split_axis=0, concat_axis=0, tiled=True)
    swapped = swapped.reshape(seq_count, expert_count, rows, column_part.shape[2])
    summed = jnp.sum(swapped.astype(jnp.float32), axis=1)
    mamba_out = jnp.transpose(summed, (1, 0, 2)).reshape(rows, -1)
    hidden = (residual.astype(jnp.float32) + mamba_out).astype(jnp.bfloat16)
    hidden_f = hidden.astype(jnp.float32)
    width_d = hidden.shape[1]
    scale_cols = width_d // BLOCK
    normed = (
        hidden_f
        * lax.rsqrt(jnp.mean(hidden_f * hidden_f, axis=-1, keepdims=True) + 1e-05)
        * norm_gain[None, :]
    )
    blocked = normed.reshape(rows, scale_cols, BLOCK)
    scales = (jnp.max(jnp.abs(blocked), axis=-1) / 448.0 + 1e-06).astype(jnp.bfloat16)
    quant = (blocked / scales.astype(jnp.float32)[..., None]).astype(jnp.bfloat16)
    restored = (
        (quant.astype(jnp.float32) * scales.astype(jnp.float32)[..., None])
        .astype(jnp.bfloat16)
        .reshape(rows, width_d)
    )
    experts = router_weight.shape[1]
    probs = jax.nn.sigmoid(jnp.dot(restored, router_weight, preferred_element_type=jnp.float32))
    picks = expert_ids[:, :, None] == jnp.arange(experts, dtype=jnp.int32)[None, None, :]
    chosen = jnp.sum(jnp.where(picks, probs[:, None, :], jnp.float32(0.0)), axis=-1)
    weights = chosen / jnp.sum(chosen, axis=-1, keepdims=True)
    coef = jnp.sum(jnp.where(expert_ids == 0, weights, jnp.float32(0.0)), axis=1)
    wanted = jnp.any(expert_ids == 0, axis=1)
    wanted_int = wanted.astype(jnp.int32)
    slot_pos = jnp.cumsum(wanted_int) - wanted_int
    capacity = rows // 2
    table = (
        (slot_pos[None, :] == jnp.arange(capacity, dtype=jnp.int32)[:, None]) & wanted[None, :]
    ).astype(jnp.bfloat16)
    send_rows = jnp.dot(table, restored, preferred_element_type=jnp.float32).astype(jnp.bfloat16)
    inputs = lax.all_gather(send_rows, ("seq", "expert"), axis=0, tiled=True)
    own_sum = lax.psum_scatter(
        expert_partial(inputs, gate_weight, up_weight, down_weight),
        ("seq", "expert"),
        scatter_dimension=0,
        tiled=True,
    )
    returned = jnp.dot(table.T, own_sum, preferred_element_type=jnp.float32)
    return (hidden_f + coef[:, None] * returned).astype(jnp.bfloat16)


def solution(mesh):
    return jax.shard_map(
        on_device,
        mesh=mesh,
        in_specs=(
            P(("dp", "seq"), "expert"),
            P(("dp", "seq"), "expert"),
            P(("dp", "seq"), "expert"),
            P("expert"),
            P(None, "expert"),
            P(None, ("dp", "seq")),
            P(None, ("dp", "seq")),
            P("expert"),
            P("expert", "seq"),
            P(("dp", "seq", "expert"), None),
            P(),
            P(),
            P(("dp", "seq", "expert"), None),
            P(None, ("seq", "expert")),
            P(None, ("seq", "expert")),
            P(("seq", "expert"), None),
        ),
        out_specs=P(("dp", "seq", "expert"), None),
        check_vma=False,
    )
```
